32 devices in a mesh: section: 4 (over y, core), expert: 8 (over z, x).
Axes of the slice: x: 2, y: 2, z: 4, core: 2. Of those that a mesh axis runs over, the one named last changes fastest.
Arguments:
- upstream: bfloat16 [4, 1024, 2048], P('section', 'expert'), may hold values from -6 to 6
- layer_input: bfloat16 [4, 1024, 2048], P('section', 'expert'), may hold values from -6 to 6
- routes: int32 [4, 1024, 2], P('section', 'expert'), may hold values from 0 to 3, all different within a row; in each aligned block of 128 rows (0 to 127, 128 to 255, ..., all dimensions but the last counted through in order) at most 128 rows name the same one
- gate_units: int32 [4, 1024, 2], P('section', 'expert'), may hold values from 1 to 256
- gate_weight: bfloat16 [4, 2048, 3072], P('section', None, 'expert'), may hold values from -0.125 to 0.125
- up_weight: bfloat16 [4, 2048, 3072], P('section', None, 'expert'), may hold values from -0.125 to 0.125
- down_weight: bfloat16 [4, 3072, 2048], P('section', 'expert'), may hold values from -0.21875 to 0.21875
Outputs:
- grad_input: bfloat16 [4, 1024, 2048], P('section', 'expert')
- grad_gate: bfloat16 [4, 2048, 3072], P('section', None, 'expert')
- grad_up: bfloat16 [4, 2048, 3072], P('section', None, 'expert')
- grad_down: bfloat16 [4, 3072, 2048], P('section', 'expert')
The draws below stay inside these ranges and needn't reach their ends.
Inputs may be any that keep to these rules, and one draw needn't show every extreme that they name: `routes`: each token names 2 different experts; in each block of 128 tokens of a section (the tokens of one device) at most 128 tokens name one expert, and in some block exactly 128 do.
All inputs are finite; a program needn't handle non-finite values.
Results may differ from the reference program's by a relative error of at most 0.0058.
Values may be sent and summed in bfloat16 or wider, within the bound.
No kernel may reach another device: no remote copies, remote signals or barrier semaphores. Data moves between devices by JAX's collectives and lax.ppermute only.
A program may use at most 128 MiB of HBM per device.

```python
import math
import jax
import jax.numpy as jnp
import numpy as np
from jax import lax

D = 2048
FF = 768
SLOTS = 2
TOK_DEV = 128
HID = 384
EXPERTS = 4
SECTIONS = 4
TOKENS = 1024
CAP = 128
N_EXPERT = 8


def place_ends(array, own_key, smallest, largest):
    shape = array.shape
    place = [jax.random.randint(jax.random.fold_in(own_key, axis), (), 0, shape[axis]) for axis in range(len(shape))]
    array = array.at[tuple(place)].set(smallest)
    longest = shape.index(max(shape))
    place[longest] = (place[longest] + 1) % shape[longest]
    return array.at[tuple(place)].set(largest)


def shard_levels(stream_key, dims, cuts, low, largest):
    level, own = 1.0, jax.random.fold_in(stream_key, 6)
    for dim, blocks in cuts:
        heights = jnp.exp(jax.random.uniform(jax.random.fold_in(own, dim), (blocks,), jnp.float32, low / len(cuts), largest / len(cuts)))
        level = level * jnp.repeat(heights, dims[dim] // blocks).reshape([-1 if axis == dim else 1 for axis in range(len(dims))])
    return level


def routed_block(own_key, own, number, rows, number_of, top, limit, lean):
    order = jax.random.permutation(own_key, number_of)
    packed, ordinary = load_shares(number_of, rows * top, limit, lean, True), load_shares(number_of, rows * top, limit, lean, False)
    places = jnp.arange(number_of)

    def named(sizes, turn):
        used = int((sizes > 0).sum())
        fixed = max(1, used // 4)
        moved = fixed + (places - fixed + turn * (used - fixed)) % max(1, number_of - fixed)
        return jnp.zeros((number_of,), jnp.int32).at[order[jnp.where(places < fixed, places, moved)]].set(jnp.asarray(sizes, jnp.int32))

    sizes = jnp.where(number % 4 == 0, named(packed, number // 4), named(ordinary, number - number // 4 - 1))
    mixed = jax.random.permutation(jax.random.fold_in(own, 3), number_of)
    giver, sink = mixed[0:number_of // 2 * 2:2], mixed[1:number_of // 2 * 2:2]
    slack = jnp.minimum(sizes[giver] - 1, limit - sizes[sink]) // 2
    slack = jnp.where((giver == order[0]) | (sink == order[0]) | (sizes[sink] == 0), 0, jnp.maximum(slack, 0))
    moved = jax.random.randint(jax.random.fold_in(own, 4), (number_of // 2,), 0, 1 << 20) % (slack + 1)
    sizes = sizes.at[giver].add(-moved).at[sink].add(moved)
    items = jnp.searchsorted(jnp.cumsum(sizes), jnp.arange(rows * top), side="right").astype(jnp.int32)
    grid = items.reshape(top, rows).T
    grid = grid[jax.random.permutation(jax.random.fold_in(own, 1), rows)]
    turn = jax.random.randint(jax.random.fold_in(own, 2), (rows, 1), 0, top)
    return jnp.take_along_axis(grid, (jnp.arange(top)[None, :] + turn) % top, axis=1)


def load_shares(count, total, most, slope, full):
    loads = [(1 << 20) // math.isqrt(rank ** slope) + 1 for rank in range(1, count + 1)]
    largest = most if full else min(most, max(-(-total // count), total * loads[0] // sum(loads)))
    least = 1 if total - largest >= count - 1 else 0
    given, rest = [largest] + [least] * (count - 1), total - largest - least * (count - 1)
    while rest > 0:
        movable = [i for i in range(1, count) if given[i] < largest] or [i for i in range(1, count) if given[i] < most]
        pool, left = sum([loads[i] for i in movable]), rest
        for i in movable:
            extra = min(most - given[i], max(1, left * loads[i] // pool), rest)
            given[i] = given[i] + extra
            rest = rest - extra
    return np.array(given)


def bell_draw(stream_key, shape, deviation, most, split=(), held_as=jnp.bfloat16):
    array = deviation * jax.random.normal(stream_key, shape, jnp.float32)
    if split:
        array = array * shard_levels(stream_key, shape, split, -0.22, 0.18)
    return jnp.clip(array, -most, most).astype(held_as)


def setup_inputs(seed: int = 0) -> dict:
    seeds = jax.random.split(jax.random.key(seed), 8)
    upstream = bell_draw(seeds[0], (SECTIONS, TOKENS, D), 1.0, 6.0, ((0, 4), (1, 8)))
    layer_input = bell_draw(seeds[1], (SECTIONS, TOKENS, D), 1.0, 6.0, ((0, 4), (1, 8)))
    routes_keys = jax.random.split(jax.random.fold_in(seeds[2], 1), SECTIONS * TOKENS // TOK_DEV)
    routes_turns = jax.random.permutation(jax.random.fold_in(seeds[2], 3), SECTIONS * TOKENS // TOK_DEV)
    routes = jax.vmap(lambda own, number: routed_block(jax.random.fold_in(seeds[2], 2), own, number, TOK_DEV, EXPERTS, SLOTS, CAP, 2))(routes_keys, routes_turns).reshape((SECTIONS, TOKENS, SLOTS))
    gate_units = place_ends(jax.random.randint(seeds[3], (SECTIONS, TOKENS, SLOTS), 1, 257), jax.random.fold_in(seeds[3], 1), 1, 256).astype(jnp.int32)
    gate_weight = bell_draw(seeds[4], (SECTIONS, D, EXPERTS * FF), D ** -0.5, 0.125, ((0, 4), (2, 8)))
    up_weight = bell_draw(seeds[5], (SECTIONS, D, EXPERTS * FF), D ** -0.5, 0.125, ((0, 4), (2, 8)))
    down_weight = bell_draw(seeds[6], (SECTIONS, EXPERTS * FF, D), FF ** -0.5, 0.21875, ((0, 4), (1, 8)))
    return {"upstream": upstream, "layer_input": layer_input, "routes": routes, "gate_units": gate_units, "gate_weight": gate_weight, "up_weight": up_weight, "down_weight": down_weight}


def expert_half(inputs, grads, w_gate, w_up, w_down):
    gate = jnp.dot(inputs, w_gate, preferred_element_type=jnp.float32)
    upper = jnp.dot(inputs, w_up, preferred_element_type=jnp.float32)
    sig = jax.nn.sigmoid(gate)
    act = gate * sig
    hidden = (act * upper).astype(jnp.bfloat16)
    dact = lax.dot_general(grads, w_down, (((1,), (1,)), ((), ())), preferred_element_type=jnp.float32)
    d_up = (dact * act).astype(jnp.bfloat16)
    d_gate = (dact * upper * sig * (1.0 + gate * (1.0 - sig))).astype(jnp.bfloat16)
    outer = (((0,), (0,)), ((), ()))
    g_down = lax.dot_general(hidden, grads, outer, preferred_element_type=jnp.float32).astype(jnp.bfloat16)
    g_gate = lax.dot_general(inputs, d_gate, outer, preferred_element_type=jnp.float32).astype(jnp.bfloat16)
    g_up = lax.dot_general(inputs, d_up, outer, preferred_element_type=jnp.float32).astype(jnp.bfloat16)
    inner = (((1,), (1,)), ((), ()))
    d_in = lax.dot_general(d_gate, w_gate, inner, preferred_element_type=jnp.float32)
    d_in = d_in + lax.dot_general(d_up, w_up, inner, preferred_element_type=jnp.float32)
    return d_in.astype(jnp.bfloat16), g_gate, g_up, g_down


def one_section(operands):
    tokens, cotangent, chosen, units, w_gate, w_up, w_down = operands
    chosen = chosen.reshape(N_EXPERT, TOK_DEV, SLOTS)
    gains = units.reshape(N_EXPERT, TOK_DEV, SLOTS).astype(jnp.float32) / 256.0
    onehot = (chosen[..., None] == jnp.arange(EXPERTS, dtype=jnp.int32)).astype(jnp.int32)
    per_token = jnp.sum(onehot, axis=2)
    before = jnp.cumsum(per_token, axis=1) - per_token
    position = jnp.sum(onehot * before[:, :, None, :], axis=3)
    source = jnp.broadcast_to(jnp.arange(N_EXPERT, dtype=jnp.int32)[:, None, None], chosen.shape)
    token_id = jnp.broadcast_to(jnp.arange(TOK_DEV, dtype=jnp.int32)[None, :, None], chosen.shape)
    table = jnp.full((EXPERTS, N_EXPERT, CAP), TOK_DEV, jnp.int32).at[chosen, source, position].set(token_id)
    weighting = jnp.zeros((EXPERTS, N_EXPERT, CAP), jnp.float32).at[chosen, source, position].set(gains)
    pad = jnp.zeros((N_EXPERT, 1, D), jnp.bfloat16)
    x_blocks = jnp.concatenate([tokens.reshape(N_EXPERT, TOK_DEV, D), pad], axis=1)
    y_blocks = jnp.concatenate([cotangent.reshape(N_EXPERT, TOK_DEV, D), pad], axis=1)
    src_index = jnp.arange(N_EXPERT, dtype=jnp.int32)[None, :, None]
    x_rows = x_blocks[src_index, table].reshape(EXPERTS, N_EXPERT * CAP, D)
    e_rows = (weighting[..., None] * y_blocks[src_index, table].astype(jnp.float32)).astype(jnp.bfloat16)
    e_rows = e_rows.reshape(EXPERTS, N_EXPERT * CAP, D)
    wg = jnp.transpose(w_gate.reshape(D, EXPERTS, 2, HID), (1, 2, 0, 3))
    wu = jnp.transpose(w_up.reshape(D, EXPERTS, 2, HID), (1, 2, 0, 3))
    wd = w_down.reshape(EXPERTS, 2, HID, D)

    def per_expert(items):
        xin, ein, gk, uk, dk = items
        first = expert_half(xin, ein, gk[0], uk[0], dk[0])
        second = expert_half(xin, ein, gk[1], uk[1], dk[1])
        summed = (first[0].astype(jnp.float32) + second[0].astype(jnp.float32)).astype(jnp.bfloat16)
        return (summed, jnp.stack([first[1], second[1]]), jnp.stack([first[2], second[2]]),
                jnp.stack([first[3], second[3]]))

    slot_grad, g_gate, g_up, g_down = lax.map(per_expert, (x_rows, e_rows, wg, wu, wd))
    slot_grad = slot_grad.reshape(EXPERTS, N_EXPERT, CAP, D)
    picked = slot_grad[chosen, source, position].astype(jnp.float32)
    total = jnp.sum(picked, axis=2) + cotangent.reshape(N_EXPERT, TOK_DEV, D).astype(jnp.float32)
    grad_input = total.astype(jnp.bfloat16).reshape(TOKENS, D)
    grad_gate = jnp.transpose(g_gate, (2, 0, 1, 3)).reshape(D, EXPERTS * FF)
    grad_up = jnp.transpose(g_up, (2, 0, 1, 3)).reshape(D, EXPERTS * FF)
    grad_down = g_down.reshape(EXPERTS * FF, D)
    return grad_input, grad_gate, grad_up, grad_down


def reference(upstream, layer_input, routes, gate_units, gate_weight, up_weight, down_weight):
    cotangent = jnp.roll(upstream, -1, axis=0)
    grad_input, grad_gate, grad_up, grad_down = lax.map(
        one_section, (layer_input, cotangent, routes, gate_units, gate_weight, up_weight, down_weight))
    return (grad_input, grad_gate, grad_up, grad_down)
```

```python
import jax
import jax.numpy as jnp
from jax import lax
from jax.sharding import PartitionSpec as P


def passed_along(value, axis, steps):
    count = lax.axis_size(axis)
    pairs = [(source, (source + steps) % count) for source in range(count)]
    return lax.ppermute(value, axis, pairs)


def expert_half(inputs, grads, w_gate, w_up, w_down):
    gate = jnp.dot(inputs, w_gate, preferred_element_type=jnp.float32)
    upper = jnp.dot(inputs, w_up, preferred_element_type=jnp.float32)
    sig = jax.nn.sigmoid(gate)
    act = gate * sig
    hidden = (act * upper).astype(jnp.bfloat16)
    dact = lax.dot_general(
        grads, w_down, (((1,), (1,)), ((), ())), preferred_element_type=jnp.float32
    )
    d_up = (dact * act).astype(jnp.bfloat16)
    d_gate = (dact * upper * sig * (1.0 + gate * (1.0 - sig))).astype(jnp.bfloat16)
    inner = (((1,), (1,)), ((), ()))
    d_in = lax.dot_general(d_gate, w_gate, inner, preferred_element_type=jnp.float32)
    d_in = d_in + lax.dot_general(d_up, w_up, inner, preferred_element_type=jnp.float32)
    outer = (((0,), (0,)), ((), ()))
    g_down = lax.dot_general(hidden, grads, outer, preferred_element_type=jnp.float32).astype(
        jnp.bfloat16
    )
    g_gate = lax.dot_general(inputs, d_gate, outer, preferred_element_type=jnp.float32).astype(
        jnp.bfloat16
    )
    g_up = lax.dot_general(inputs, d_up, outer, preferred_element_type=jnp.float32).astype(
        jnp.bfloat16
    )
    return (d_in.astype(jnp.bfloat16), g_gate, g_up, g_down)


def shards(upstream, layer_input, routes, gate_units, gate_weight, up_weight, down_weight):
    received = passed_along(upstream, "section", -1)[0]
    tokens = layer_input[0]
    expert = lax.axis_index("expert") // 2
    all_tokens = lax.all_gather(tokens, "expert", axis=0, tiled=True)
    all_grads = lax.all_gather(received, "expert", axis=0, tiled=True)
    all_routes = lax.all_gather(routes[0], "expert", axis=0, tiled=True)
    all_units = lax.all_gather(gate_units[0], "expert", axis=0, tiled=True)
    gains = jnp.sum(
        jnp.where(all_routes == expert, all_units.astype(jnp.float32) / 256.0, 0.0), axis=1
    )
    weighted = (gains[:, None] * all_grads.astype(jnp.float32)).astype(jnp.bfloat16)
    d_in, g_gate, g_up, g_down = expert_half(
        all_tokens, weighted, gate_weight[0], up_weight[0], down_weight[0]
    )
    summed = lax.psum_scatter(
        d_in.astype(jnp.float32), "expert", scatter_dimension=0, tiled=True
    )
    grad_input = (summed + received.astype(jnp.float32)).astype(jnp.bfloat16)
    return (grad_input[None], g_gate[None], g_up[None], g_down[None])


def solution(mesh):
    in_specs = (
        P("section", "expert", None),
        P("section", "expert", None),
        P("section", "expert", None),
        P("section", "expert", None),
        P("section", None, "expert"),
        P("section", None, "expert"),
        P("section", "expert", None),
    )
    out_specs = (
        P("section", "expert", None),
        P("section", None, "expert"),
        P("section", None, "expert"),
        P("section", "expert", None),
    )
    return jax.shard_map(shards, mesh=mesh, in_specs=in_specs, out_specs=out_specs, check_vma=False)
```

```python
import jax
import jax.numpy as jnp
from jax import lax
from jax.sharding import PartitionSpec as P


def passed_along(value, axis, steps):
    count = lax.axis_size(axis)
    pairs = [(source, (source + steps) % count) for source in range(count)]
    return lax.ppermute(value, axis, pairs)


def ring_order(count):
    half = count // 2
    return [2 * a for a in range(half)] + [2 * a + 1 for a in reversed(range(half))]


def along_ring(value, ring, steps):
    count = len(ring)
    pairs = [(ring[i], ring[(i + steps) % count]) for i in range(count)]
    return lax.ppermute(value, "expert", pairs)


def expert_rows(inputs, grads, w_gate, w_up, w_down):
    gate = jnp.dot(inputs, w_gate, preferred_element_type=jnp.float32)
    upper = jnp.dot(inputs, w_up, preferred_element_type=jnp.float32)
    sig = jax.nn.sigmoid(gate)
    act = gate * sig
    hidden = (act * upper).astype(jnp.bfloat16)
    dact = lax.dot_general(
        grads, w_down, (((1,), (1,)), ((), ())), preferred_element_type=jnp.float32
    )
    d_up = (dact * act).astype(jnp.bfloat16)
    d_gate = (dact * upper * sig * (1.0 + gate * (1.0 - sig))).astype(jnp.bfloat16)
    inner = (((1,), (1,)), ((), ()))
    d_in = lax.dot_general(d_gate, w_gate, inner, preferred_element_type=jnp.float32)
    d_in = d_in + lax.dot_general(d_up, w_up, inner, preferred_element_type=jnp.float32)
    outer = (((0,), (0,)), ((), ()))
    g_down = lax.dot_general(hidden, grads, outer, preferred_element_type=jnp.float32)
    g_gate = lax.dot_general(inputs, d_gate, outer, preferred_element_type=jnp.float32)
    g_up = lax.dot_general(inputs, d_up, outer, preferred_element_type=jnp.float32)
    return d_in.astype(jnp.bfloat16), g_gate, g_up, g_down


def shards(upstream, layer_input, routes, gate_units, gate_weight, up_weight, down_weight):
    received = passed_along(upstream, "section", -1)[0]
    tokens = layer_input[0]
    tok_rows, width = tokens.shape
    count = lax.axis_size("expert")
    experts = count // 2
    expert = lax.axis_index("expert") // 2
    ring = ring_order(count)
    lanes = 128
    units = gate_units[0].astype(jnp.float32) / 256.0
    chosen = routes[0][:, :, None] == jnp.arange(lanes, dtype=jnp.int32)[None, None, :]
    gains = jnp.sum(jnp.where(chosen, units[:, :, None], 0.0), axis=1).astype(jnp.bfloat16)
    packed = jnp.concatenate([tokens, received, gains], axis=1)
    rows = tok_rows // 2
    w_gate, w_up, w_down = gate_weight[0], up_weight[0], down_weight[0]
    pick = (jnp.arange(lanes, dtype=jnp.int32) == expert).astype(jnp.float32)

    def contribution(ahead, behind):
        block = jnp.concatenate([ahead, behind], axis=0)
        inputs = block[:, :width]
        grads = block[:, width : 2 * width].astype(jnp.float32)
        gain = jnp.sum(block[:, 2 * width :].astype(jnp.float32) * pick[None, :], axis=1)
        weighted = (gain[:, None] * grads).astype(jnp.bfloat16)
        part, g_gate, g_up, g_down = expert_rows(inputs, weighted, w_gate, w_up, w_down)
        part = part.astype(jnp.float32)
        return (part[:rows], part[rows:]), (g_gate, g_up, g_down)

    ahead, behind = packed[:rows], packed[rows:]
    next_ahead, next_behind = along_ring(ahead, ring, 1), along_ring(behind, ring, -1)
    parts, acc = contribution(ahead, behind)
    ahead, behind = next_ahead, next_behind
    trail = (jnp.zeros_like(parts[0]), jnp.zeros_like(parts[1]))

    def step(_, carry):
        ahead, behind, parts, trail, acc = carry
        sums = (trail[0] + parts[0], trail[1] + parts[1])
        sent = (along_ring(sums[0], ring, 1), along_ring(sums[1], ring, -1))
        next_ahead, next_behind = along_ring(ahead, ring, 1), along_ring(behind, ring, -1)
        parts, grads = contribution(ahead, behind)
        acc = tuple(a + g for a, g in zip(acc, grads))
        return next_ahead, next_behind, parts, sent, acc

    ahead, behind, parts, trail, acc = lax.fori_loop(
        1, count - 1, step, (ahead, behind, parts, trail, acc)
    )
    sums = (trail[0] + parts[0], trail[1] + parts[1])
    sent = (along_ring(sums[0], ring, 1), along_ring(sums[1], ring, -1))
    parts, grads = contribution(ahead, behind)
    acc = tuple(a + g for a, g in zip(acc, grads))
    trail = sent
    sums = (trail[0] + parts[0], trail[1] + parts[1])
    total = jnp.concatenate([along_ring(sums[0], ring, 1), along_ring(sums[1], ring, -1)], axis=0)
    grad_input = (total + received.astype(jnp.float32)).astype(jnp.bfloat16)
    g_gate, g_up, g_down = (a.astype(jnp.bfloat16) for a in acc)
    return (grad_input[None], g_gate[None], g_up[None], g_down[None])


def solution(mesh):
    in_specs = (
        P("section", "expert", None),
        P("section", "expert", None),
        P("section", "expert", None),
        P("section", "expert", None),
        P("section", None, "expert"),
        P("section", None, "expert"),
        P("section", "expert", None),
    )
    out_specs = (
        P("section", "expert", None),
        P("section", None, "expert"),
        P("section", None, "expert"),
        P("section", "expert", None),
    )
    return jax.shard_map(shards, mesh=mesh, in_specs=in_specs, out_specs=out_specs, check_vma=False)
```

```python
import jax
import jax.numpy as jnp
from jax import lax
from jax.sharding import PartitionSpec as P


def passed_along(value, axis, steps):
    count = lax.axis_size(axis)
    pairs = [(source, (source + steps) % count) for source in range(count)]
    return lax.ppermute(value, axis, pairs)


def ring_order(count):
    half = count // 2
    return [2 * a for a in range(half)] + [2 * a + 1 for a in reversed(range(half))]


def along_ring(value, ring, steps):
    count = len(ring)
    pairs = [(ring[i], ring[(i + steps) % count]) for i in range(count)]
    return lax.ppermute(value, "expert", pairs)


def expert_rows(inputs, grads, w_gate, w_up):
    gate = jnp.dot(inputs, w_gate, preferred_element_type=jnp.float32)
    upper = jnp.dot(inputs, w_up, preferred_element_type=jnp.float32)
    return gate, upper


def row_grads(inputs, grads, w_gate, w_up, w_down):
    gate, upper = expert_rows(inputs, grads, w_gate, w_up)
    sig = jax.nn.sigmoid(gate)
    act = gate * sig
    hidden = (act * upper).astype(jnp.bfloat16)
    dact = lax.dot_general(
        grads, w_down, (((1,), (1,)), ((), ())), preferred_element_type=jnp.float32
    )
    d_up = (dact * act).astype(jnp.bfloat16)
    d_gate = (dact * upper * sig * (1.0 + gate * (1.0 - sig))).astype(jnp.bfloat16)
    inner = (((1,), (1,)), ((), ()))
    d_in = lax.dot_general(d_gate, w_gate, inner, preferred_element_type=jnp.float32)
    d_in = d_in + lax.dot_general(d_up, w_up, inner, preferred_element_type=jnp.float32)
    return d_in.astype(jnp.bfloat16), hidden, d_gate, d_up


def shards(upstream, layer_input, routes, gate_units, gate_weight, up_weight, down_weight):
    received = passed_along(upstream, "section", -1)[0]
    tokens = layer_input[0]
    tok_rows, width = tokens.shape
    count = lax.axis_size("expert")
    experts = count // 2
    expert = lax.axis_index("expert") // 2
    ring = ring_order(count)
    lanes = 128
    units = gate_units[0].astype(jnp.float32) / 256.0
    chosen = routes[0][:, :, None] == jnp.arange(lanes, dtype=jnp.int32)[None, None, :]
    gains = jnp.sum(jnp.where(chosen, units[:, :, None], 0.0), axis=1).astype(jnp.bfloat16)
    packed = jnp.concatenate([tokens, received, gains], axis=1)
    rows = tok_rows // 2
    w_gate, w_up, w_down = gate_weight[0], up_weight[0], down_weight[0]
    pick = (jnp.arange(lanes, dtype=jnp.int32) == expert).astype(jnp.float32)

    kept = []
    sums = None
    ahead, behind = packed[:rows], packed[rows:]
    for step in range(count):
        if step > 0:
            ahead = along_ring(ahead, ring, 1)
            behind = along_ring(behind, ring, -1)
            sums = (along_ring(sums[0], ring, 1), along_ring(sums[1], ring, -1))
        block = jnp.concatenate([ahead, behind], axis=0)
        inputs = block[:, :width]
        grads = block[:, width : 2 * width].astype(jnp.float32)
        gain = jnp.sum(block[:, 2 * width :].astype(jnp.float32) * pick[None, :], axis=1)
        weighted = (gain[:, None] * grads).astype(jnp.bfloat16)
        part, hidden, d_gate, d_up = row_grads(inputs, weighted, w_gate, w_up, w_down)
        part = part.astype(jnp.float32)
        if sums is None:
            sums = (part[:rows], part[rows:])
        else:
            sums = (sums[0] + part[:rows], sums[1] + part[rows:])
        kept.append((inputs, weighted, hidden, d_gate, d_up))
    total = jnp.concatenate([along_ring(sums[0], ring, 1), along_ring(sums[1], ring, -1)], axis=0)
    inputs, weighted, hidden, d_gate, d_up = (
        jnp.concatenate([k[i] for k in kept], axis=0) for i in range(5)
    )
    outer = (((0,), (0,)), ((), ()))
    g_down = lax.dot_general(hidden, weighted, outer, preferred_element_type=jnp.float32)
    g_gate = lax.dot_general(inputs, d_gate, outer, preferred_element_type=jnp.float32)
    g_up = lax.dot_general(inputs, d_up, outer, preferred_element_type=jnp.float32)
    acc = (g_gate, g_up, g_down)
    grad_input = (total + received.astype(jnp.float32)).astype(jnp.bfloat16)
    g_gate, g_up, g_down = (a.astype(jnp.bfloat16) for a in acc)
    return (grad_input[None], g_gate[None], g_up[None], g_down[None])


def solution(mesh):
    in_specs = (
        P("section", "expert", None),
        P("section", "expert", None),
        P("section", "expert", None),
        P("section", "expert", None),
        P("section", None, "expert"),
        P("section", None, "expert"),
        P("section", "expert", None),
    )
    out_specs = (
        P("section", "expert", None),
        P("section", None, "expert"),
        P("section", None, "expert"),
        P("section", "expert", None),
    )
    return jax.shard_map(shards, mesh=mesh, in_specs=in_specs, out_specs=out_specs, check_vma=False)
```

```python
import jax
import jax.numpy as jnp
from jax import lax
from jax.sharding import PartitionSpec as P


def passed_along(value, axis, steps):
    count = lax.axis_size(axis)
    pairs = [(source, (source + steps) % count) for source in range(count)]
    return lax.ppermute(value, axis, pairs)


def ring_order(count):
    half = count // 2
    return [2 * a for a in range(half)] + [2 * a + 1 for a in reversed(range(half))]


def along_ring(value, ring, steps):
    count = len(ring)
    pairs = [(ring[i], ring[(i + steps) % count]) for i in range(count)]
    return lax.ppermute(value, "expert", pairs)


def expert_rows(inputs, grads, w_gate, w_up):
    gate = jnp.dot(inputs, w_gate, preferred_element_type=jnp.float32)
    upper = jnp.dot(inputs, w_up, preferred_element_type=jnp.float32)
    return gate, upper


def row_grads(inputs, grads, w_gate, w_up, w_down):
    gate, upper = expert_rows(inputs, grads, w_gate, w_up)
    sig = jax.nn.sigmoid(gate)
    act = gate * sig
    hidden = (act * upper).astype(jnp.bfloat16)
    dact = lax.dot_general(
        grads, w_down, (((1,), (1,)), ((), ())), preferred_element_type=jnp.float32
    )
    d_up = (dact * act).astype(jnp.bfloat16)
    d_gate = (dact * upper * sig * (1.0 + gate * (1.0 - sig))).astype(jnp.bfloat16)
    inner = (((1,), (1,)), ((), ()))
    d_in = lax.dot_general(d_gate, w_gate, inner, preferred_element_type=jnp.float32)
    d_in = d_in + lax.dot_general(d_up, w_up, inner, preferred_element_type=jnp.float32)
    return d_in.astype(jnp.bfloat16), hidden, d_gate, d_up


def shards(upstream, layer_input, routes, gate_units, gate_weight, up_weight, down_weight):
    received = passed_along(upstream, "section", -1)[0]
    tokens = layer_input[0]
    tok_rows, width = tokens.shape
    count = lax.axis_size("expert")
    experts = count // 2
    expert = lax.axis_index("expert") // 2
    ring = ring_order(count)
    lanes = 128
    units = gate_units[0].astype(jnp.float32) / 256.0
    chosen = routes[0][:, :, None] == jnp.arange(lanes, dtype=jnp.int32)[None, None, :]
    gains = jnp.sum(jnp.where(chosen, units[:, :, None], 0.0), axis=1).astype(jnp.bfloat16)
    packed = jnp.concatenate([tokens, received, gains], axis=1)
    rows = tok_rows // 2
    w_gate, w_up, w_down = gate_weight[0], up_weight[0], down_weight[0]
    pick = (jnp.arange(lanes, dtype=jnp.int32) == expert).astype(jnp.float32)

    kept = []
    sums = None
    ahead, behind = packed[:rows], packed[rows:]
    for step in range(count):
        if step > 0:
            ahead = along_ring(ahead, ring, 1)
            behind = along_ring(behind, ring, -1)
            sums = (along_ring(sums[0], ring, 1), along_ring(sums[1], ring, -1))
        block = jnp.concatenate([ahead, behind], axis=0)
        inputs = block[:, :width]
        grads = block[:, width : 2 * width].astype(jnp.float32)
        gain = jnp.sum(block[:, 2 * width :].astype(jnp.float32) * pick[None, :], axis=1)
        weighted = (gain[:, None] * grads).astype(jnp.bfloat16)
        part, hidden, d_gate, d_up = row_grads(inputs, weighted, w_gate, w_up, w_down)
        if sums is None:
            sums = (part[:rows], part[rows:])
        else:
            sums = (
                (sums[0].astype(jnp.float32) + part[:rows].astype(jnp.float32)).astype(jnp.bfloat16),
                (sums[1].astype(jnp.float32) + part[rows:].astype(jnp.float32)).astype(jnp.bfloat16),
            )
        kept.append((inputs, weighted, hidden, d_gate, d_up))
    total = jnp.concatenate([along_ring(sums[0], ring, 1), along_ring(sums[1], ring, -1)], axis=0)
    inputs, weighted, hidden, d_gate, d_up = (
        jnp.concatenate([k[i] for k in kept], axis=0) for i in range(5)
    )
    outer = (((0,), (0,)), ((), ()))
    g_down = lax.dot_general(hidden, weighted, outer, preferred_element_type=jnp.float32)
    g_gate = lax.dot_general(inputs, d_gate, outer, preferred_element_type=jnp.float32)
    g_up = lax.dot_general(inputs, d_up, outer, preferred_element_type=jnp.float32)
    acc = (g_gate, g_up, g_down)
    grad_input = (total.astype(jnp.float32) + received.astype(jnp.float32)).astype(jnp.bfloat16)
    g_gate, g_up, g_down = (a.astype(jnp.bfloat16) for a in acc)
    return (grad_input[None], g_gate[None], g_up[None], g_down[None])


def solution(mesh):
    in_specs = (
        P("section", "expert", None),
        P("section", "expert", None),
        P("section", "expert", None),
        P("section", "expert", None),
        P("section", None, "expert"),
        P("section", None, "expert"),
        P("section", "expert", None),
    )
    out_specs = (
        P("section", "expert", None),
        P("section", None, "expert"),
        P("section", None, "expert"),
        P("section", "expert", None),
    )
    return jax.shard_map(shards, mesh=mesh, in_specs=in_specs, out_specs=out_specs, check_vma=False)
```

```python
import jax
import jax.numpy as jnp
from jax import lax
from jax.sharding import PartitionSpec as P


def passed_along(value, axis, steps):
    count = lax.axis_size(axis)
    pairs = [(source, (source + steps) % count) for source in range(count)]
    return lax.ppermute(value, axis, pairs)


def ring_order(count):
    half = count // 2
    return [2 * a for a in range(half)] + [2 * a + 1 for a in reversed(range(half))]


def along_ring(value, ring, steps):
    count = len(ring)
    pairs = [(ring[i], ring[(i + steps) % count]) for i in range(count)]
    return lax.ppermute(value, "expert", pairs)


def expert_rows(inputs, grads, w_gate, w_up):
    gate = jnp.dot(inputs, w_gate, preferred_element_type=jnp.float32)
    upper = jnp.dot(inputs, w_up, preferred_element_type=jnp.float32)
    return gate, upper


def row_grads(inputs, grads, w_gate, w_up, w_down):
    gate, upper = expert_rows(inputs, grads, w_gate, w_up)
    sig = jax.nn.sigmoid(gate)
    act = gate * sig
    hidden = (act * upper).astype(jnp.bfloat16)
    dact = lax.dot_general(
        grads, w_down, (((1,), (1,)), ((), ())), preferred_element_type=jnp.float32
    )
    d_up = (dact * act).astype(jnp.bfloat16)
    d_gate = (dact * upper * sig * (1.0 + gate * (1.0 - sig))).astype(jnp.bfloat16)
    inner = (((1,), (1,)), ((), ()))
    d_in = lax.dot_general(d_gate, w_gate, inner, preferred_element_type=jnp.float32)
    d_in = d_in + lax.dot_general(d_up, w_up, inner, preferred_element_type=jnp.float32)
    return d_in.astype(jnp.bfloat16), hidden, d_gate, d_up


def shards(upstream, layer_input, routes, gate_units, gate_weight, up_weight, down_weight):
    received = passed_along(upstream, "section", -1)[0]
    tokens = layer_input[0]
    tok_rows, width = tokens.shape
    count = lax.axis_size("expert")
    experts = count // 2
    expert = lax.axis_index("expert") // 2
    ring = ring_order(count)
    lanes = 128
    units = gate_units[0].astype(jnp.float32) / 256.0
    chosen = routes[0][:, :, None] == jnp.arange(lanes, dtype=jnp.int32)[None, None, :]
    gains = jnp.sum(jnp.where(chosen, units[:, :, None], 0.0), axis=1).astype(jnp.bfloat16)
    packed = jnp.concatenate([tokens, received, gains], axis=1)
    rows = tok_rows // 2
    w_gate, w_up, w_down = gate_weight[0], up_weight[0], down_weight[0]
    pick = (jnp.arange(lanes, dtype=jnp.int32) == expert).astype(jnp.float32)

    data = packed.shape[1]

    def contribution(block):
        inputs = block[:, :width]
        grads = block[:, width : 2 * width].astype(jnp.float32)
        gain = jnp.sum(block[:, 2 * width : data].astype(jnp.float32) * pick[None, :], axis=1)
        weighted = (gain[:, None] * grads).astype(jnp.bfloat16)
        part, hidden, d_gate, d_up = row_grads(inputs, weighted, w_gate, w_up, w_down)
        kept.append((inputs, weighted, hidden, d_gate, d_up))
        return part[:rows], part[rows:]

    def added(trail, part):
        return (trail.astype(jnp.float32) + part.astype(jnp.float32)).astype(jnp.bfloat16)

    kept = []
    ahead, behind = packed[:rows], packed[rows:]
    sent_ahead, sent_behind = along_ring(ahead, ring, 1), along_ring(behind, ring, -1)
    parts = contribution(packed)
    for step in range(1, count):
        ahead, behind = sent_ahead, sent_behind
        if step == 1:
            sums = parts
        else:
            trail = (ahead[:, data:], behind[:, data:])
            sums = (added(trail[0], parts[0]), added(trail[1], parts[1]))
        if step < count - 1:
            sent_ahead = along_ring(jnp.concatenate([ahead[:, :data], sums[0]], axis=1), ring, 1)
            sent_behind = along_ring(jnp.concatenate([behind[:, :data], sums[1]], axis=1), ring, -1)
        else:
            sent_ahead = along_ring(sums[0], ring, 1)
            sent_behind = along_ring(sums[1], ring, -1)
        parts = contribution(jnp.concatenate([ahead[:, :data], behind[:, :data]], axis=0))
    trail = (sent_ahead, sent_behind)
    sums = (added(trail[0], parts[0]), added(trail[1], parts[1]))
    total = jnp.concatenate([along_ring(sums[0], ring, 1), along_ring(sums[1], ring, -1)], axis=0)
    inputs, weighted, hidden, d_gate, d_up = (
        jnp.concatenate([k[i] for k in kept], axis=0) for i in range(5)
    )
    outer = (((0,), (0,)), ((), ()))
    g_down = lax.dot_general(hidden, weighted, outer, preferred_element_type=jnp.float32)
    g_gate = lax.dot_general(inputs, d_gate, outer, preferred_element_type=jnp.float32)
    g_up = lax.dot_general(inputs, d_up, outer, preferred_element_type=jnp.float32)
    acc = (g_gate, g_up, g_down)
    grad_input = (total.astype(jnp.float32) + received.astype(jnp.float32)).astype(jnp.bfloat16)
    g_gate, g_up, g_down = (a.astype(jnp.bfloat16) for a in acc)
    return (grad_input[None], g_gate[None], g_up[None], g_down[None])


def solution(mesh):
    in_specs = (
        P("section", "expert", None),
        P("section", "expert", None),
        P("section", "expert", None),
        P("section", "expert", None),
        P("section", None, "expert"),
        P("section", None, "expert"),
        P("section", "expert", None),
    )
    out_specs = (
        P("section", "expert", None),
        P("section", None, "expert"),
        P("section", None, "expert"),
        P("section", "expert", None),
    )
    return jax.shard_map(shards, mesh=mesh, in_specs=in_specs, out_specs=out_specs, check_vma=False)
```

```python
import jax
import jax.numpy as jnp
from jax import lax
from jax.sharding import PartitionSpec as P


def passed_along(value, axis, steps):
    count = lax.axis_size(axis)
    pairs = [(source, (source + steps) % count) for source in range(count)]
    return lax.ppermute(value, axis, pairs)


def ring_order(count):
    half = count // 2
    return [2 * a for a in range(half)] + [2 * a + 1 for a in reversed(range(half))]


def along_ring(value, ring, steps):
    count = len(ring)
    pairs = [(ring[i], ring[(i + steps) % count]) for i in range(count)]
    return lax.ppermute(value, "expert", pairs)


def expert_rows(inputs, grads, w_gate, w_up):
    gate = jnp.dot(inputs, w_gate, preferred_element_type=jnp.float32)
    upper = jnp.dot(inputs, w_up, preferred_element_type=jnp.float32)
    return gate, upper


def row_grads(inputs, grads, w_gate, w_up, w_down):
    gate, upper = expert_rows(inputs, grads, w_gate, w_up)
    sig = jax.nn.sigmoid(gate)
    act = gate * sig
    hidden = (act * upper).astype(jnp.bfloat16)
    dact = lax.dot_general(
        grads, w_down, (((1,), (1,)), ((), ())), preferred_element_type=jnp.float32
    )
    d_up = (dact * act).astype(jnp.bfloat16)
    d_gate = (dact * upper * sig * (1.0 + gate * (1.0 - sig))).astype(jnp.bfloat16)
    inner = (((1,), (1,)), ((), ()))
    d_in = lax.dot_general(d_gate, w_gate, inner, preferred_element_type=jnp.float32)
    d_in = d_in + lax.dot_general(d_up, w_up, inner, preferred_element_type=jnp.float32)
    return d_in.astype(jnp.bfloat16), hidden, d_gate, d_up


def shards(upstream, layer_input, routes, gate_units, gate_weight, up_weight, down_weight):
    received = passed_along(upstream, "section", -1)[0]
    tokens = layer_input[0]
    tok_rows, width = tokens.shape
    count = lax.axis_size("expert")
    experts = count // 2
    expert = lax.axis_index("expert") // 2
    ring = ring_order(count)
    lanes = 128
    units = gate_units[0].astype(jnp.float32) / 256.0
    chosen = routes[0][:, :, None] == jnp.arange(lanes, dtype=jnp.int32)[None, None, :]
    gains = jnp.sum(jnp.where(chosen, units[:, :, None], 0.0), axis=1).astype(jnp.bfloat16)
    packed = jnp.concatenate([tokens, received, gains], axis=1)
    rows = tok_rows // 2
    w_gate, w_up, w_down = gate_weight[0], up_weight[0], down_weight[0]
    pick = (jnp.arange(lanes, dtype=jnp.int32) == expert).astype(jnp.float32)

    data = packed.shape[1]

    def contribution(block):
        inputs = block[:, :width]
        grads = block[:, width : 2 * width].astype(jnp.float32)
        gain = jnp.sum(block[:, 2 * width : data].astype(jnp.float32) * pick[None, :], axis=1)
        weighted = (gain[:, None] * grads).astype(jnp.bfloat16)
        part, hidden, d_gate, d_up = row_grads(inputs, weighted, w_gate, w_up, w_down)
        kept.append((inputs, weighted, hidden, d_gate, d_up))
        return part[:rows], part[rows:]

    def added(trail, part):
        return (trail.astype(jnp.float32) + part.astype(jnp.float32)).astype(jnp.bfloat16)

    kept = []
    ahead, behind = packed[:rows], packed[rows:]
    sent_ahead, sent_behind = along_ring(ahead, ring, 1), along_ring(behind, ring, -1)
    parts = contribution(packed)
    for step in range(1, count):
        ahead, behind = sent_ahead, sent_behind
        if step == 1:
            sums = parts
        else:
            trail = (ahead[:, data:], behind[:, data:])
            sums = (added(trail[0], parts[0]), added(trail[1], parts[1]))
        if step < count - 1:
            sent_ahead = along_ring(jnp.concatenate([ahead[:, :data], sums[0]], axis=1), ring, 1)
            sent_behind = along_ring(jnp.concatenate([behind[:, :data], sums[1]], axis=1), ring, -1)
        else:
            sent_ahead = along_ring(sums[0], ring, 1)
            sent_behind = along_ring(sums[1], ring, -1)
        parts = contribution(jnp.concatenate([ahead[:, :data], behind[:, :data]], axis=0))
    trail = (sent_ahead, sent_behind)
    sums = (added(trail[0], parts[0]), added(trail[1], parts[1]))
    total = jnp.concatenate([along_ring(sums[0], ring, 1), along_ring(sums[1], ring, -1)], axis=0)
    outer = (((0,), (0,)), ((), ()))
    acc = None
    for first, last in ((0, count // 2), (count // 2, count - 1), (count - 1, count)):
        inputs, weighted, hidden, d_gate, d_up = (
            jnp.concatenate([k[i] for k in kept[first:last]], axis=0) for i in range(5)
        )
        grads = (
            lax.dot_general(inputs, d_gate, outer, preferred_element_type=jnp.float32),
            lax.dot_general(inputs, d_up, outer, preferred_element_type=jnp.float32),
            lax.dot_general(hidden, weighted, outer, preferred_element_type=jnp.float32),
        )
        acc = grads if acc is None else tuple(a + g for a, g in zip(acc, grads))
    grad_input = (total.astype(jnp.float32) + received.astype(jnp.float32)).astype(jnp.bfloat16)
    g_gate, g_up, g_down = (a.astype(jnp.bfloat16) for a in acc)
    return (grad_input[None], g_gate[None], g_up[None], g_down[None])


def solution(mesh):
    in_specs = (
        P("section", "expert", None),
        P("section", "expert", None),
        P("section", "expert", None),
        P("section", "expert", None),
        P("section", None, "expert"),
        P("section", None, "expert"),
        P("section", "expert", None),
    )
    out_specs = (
        P("section", "expert", None),
        P("section", None, "expert"),
        P("section", None, "expert"),
        P("section", "expert", None),
    )
    return jax.shard_map(shards, mesh=mesh, in_specs=in_specs, out_specs=out_specs, check_vma=False)
```

```python
import jax
import jax.numpy as jnp
from jax import lax
from jax.sharding import PartitionSpec as P


def passed_along(value, axis, steps):
    count = lax.axis_size(axis)
    pairs = [(source, (source + steps) % count) for source in range(count)]
    return lax.ppermute(value, axis, pairs)


def ring_order(count):
    half = count // 2
    return [2 * a for a in range(half)] + [2 * a + 1 for a in reversed(range(half))]


def along_ring(value, ring, steps):
    count = len(ring)
    pairs = [(ring[i], ring[(i + steps) % count]) for i in range(count)]
    return lax.ppermute(value, "expert", pairs)


def expert_rows(inputs, grads, w_gate, w_up):
    gate = jnp.dot(inputs, w_gate, preferred_element_type=jnp.float32)
    upper = jnp.dot(inputs, w_up, preferred_element_type=jnp.float32)
    return gate, upper


def row_grads(inputs, grads, w_gate, w_up, w_down):
    gate, upper = expert_rows(inputs, grads, w_gate, w_up)
    sig = jax.nn.sigmoid(gate)
    act = gate * sig
    hidden = (act * upper).astype(jnp.bfloat16)
    dact = lax.dot_general(
        grads, w_down, (((1,), (1,)), ((), ())), preferred_element_type=jnp.float32
    )
    d_up = (dact * act).astype(jnp.bfloat16)
    d_gate = (dact * upper * sig * (1.0 + gate * (1.0 - sig))).astype(jnp.bfloat16)
    inner = (((1,), (1,)), ((), ()))
    d_in = lax.dot_general(d_gate, w_gate, inner, preferred_element_type=jnp.float32)
    d_in = d_in + lax.dot_general(d_up, w_up, inner, preferred_element_type=jnp.float32)
    return d_in.astype(jnp.bfloat16), hidden, d_gate, d_up


def shards(upstream, layer_input, routes, gate_units, gate_weight, up_weight, down_weight):
    received = passed_along(upstream, "section", -1)[0]
    tokens = layer_input[0]
    tok_rows, width = tokens.shape
    count = lax.axis_size("expert")
    experts = count // 2
    expert = lax.axis_index("expert") // 2
    ring = ring_order(count)
    lanes = 128
    units = gate_units[0].astype(jnp.float32) / 256.0
    chosen = routes[0][:, :, None] == jnp.arange(lanes, dtype=jnp.int32)[None, None, :]
    gains = jnp.sum(jnp.where(chosen, units[:, :, None], 0.0), axis=1).astype(jnp.bfloat16)
    packed = jnp.concatenate([tokens, received, gains], axis=1)
    early = jnp.concatenate([tokens, gains], axis=1)
    rows = tok_rows // 2
    w_gate, w_up, w_down = gate_weight[0], up_weight[0], down_weight[0]
    pick = (jnp.arange(lanes, dtype=jnp.int32) == expert).astype(jnp.float32)

    data = packed.shape[1]

    def contribution(block):
        inputs = block[:, :width]
        grads = block[:, width : 2 * width].astype(jnp.float32)
        gain = jnp.sum(block[:, 2 * width : data].astype(jnp.float32) * pick[None, :], axis=1)
        weighted = (gain[:, None] * grads).astype(jnp.bfloat16)
        part, hidden, d_gate, d_up = row_grads(inputs, weighted, w_gate, w_up, w_down)
        kept.append((inputs, weighted, hidden, d_gate, d_up))
        return part[:rows], part[rows:]

    def added(trail, part):
        return (trail.astype(jnp.float32) + part.astype(jnp.float32)).astype(jnp.bfloat16)

    kept = []
    ahead, behind = packed[:rows], packed[rows:]
    early_ahead = along_ring(early[:rows], ring, 1)
    early_behind = along_ring(early[rows:], ring, -1)
    late_ahead = along_ring(received[:rows], ring, 1)
    late_behind = along_ring(received[rows:], ring, -1)
    parts = contribution(packed)
    for step in range(1, count):
        if step == 1:
            ahead, behind = (
                jnp.concatenate([e[:, :width], l, e[:, width:]], axis=1)
                for e, l in ((early_ahead, late_ahead), (early_behind, late_behind))
            )
        else:
            ahead, behind = sent_ahead, sent_behind
        if step == 1:
            sums = parts
        else:
            trail = (ahead[:, data:], behind[:, data:])
            sums = (added(trail[0], parts[0]), added(trail[1], parts[1]))
        if step < count - 1:
            sent_ahead = along_ring(jnp.concatenate([ahead[:, :data], sums[0]], axis=1), ring, 1)
            sent_behind = along_ring(jnp.concatenate([behind[:, :data], sums[1]], axis=1), ring, -1)
        else:
            sent_ahead = along_ring(sums[0], ring, 1)
            sent_behind = along_ring(sums[1], ring, -1)
        parts = contribution(jnp.concatenate([ahead[:, :data], behind[:, :data]], axis=0))
    trail = (sent_ahead, sent_behind)
    sums = (added(trail[0], parts[0]), added(trail[1], parts[1]))
    total = jnp.concatenate([along_ring(sums[0], ring, 1), along_ring(sums[1], ring, -1)], axis=0)
    outer = (((0,), (0,)), ((), ()))
    acc = None
    for first, last in ((0, count // 2), (count // 2, count - 1), (count - 1, count)):
        inputs, weighted, hidden, d_gate, d_up = (
            jnp.concatenate([k[i] for k in kept[first:last]], axis=0) for i in range(5)
        )
        grads = (
            lax.dot_general(inputs, d_gate, outer, preferred_element_type=jnp.float32),
            lax.dot_general(inputs, d_up, outer, preferred_element_type=jnp.float32),
            lax.dot_general(hidden, weighted, outer, preferred_element_type=jnp.float32),
        )
        acc = grads if acc is None else tuple(a + g for a, g in zip(acc, grads))
    grad_input = (total.astype(jnp.float32) + received.astype(jnp.float32)).astype(jnp.bfloat16)
    g_gate, g_up, g_down = (a.astype(jnp.bfloat16) for a in acc)
    return (grad_input[None], g_gate[None], g_up[None], g_down[None])


def solution(mesh):
    in_specs = (
        P("section", "expert", None),
        P("section", "expert", None),
        P("section", "expert", None),
        P("section", "expert", None),
        P("section", None, "expert"),
        P("section", None, "expert"),
        P("section", "expert", None),
    )
    out_specs = (
        P("section", "expert", None),
        P("section", None, "expert"),
        P("section", None, "expert"),
        P("section", "expert", None),
    )
    return jax.shard_map(shards, mesh=mesh, in_specs=in_specs, out_specs=out_specs, check_vma=False)
```

```python
import jax
import jax.numpy as jnp
from jax import lax
from jax.sharding import PartitionSpec as P


def passed_along(value, axis, steps):
    count = lax.axis_size(axis)
    pairs = [(source, (source + steps) % count) for source in range(count)]
    return lax.ppermute(value, axis, pairs)


def ring_order(count):
    half = count // 2
    return [2 * a for a in range(half)] + [2 * a + 1 for a in reversed(range(half))]


def along_ring(value, ring, steps):
    count = len(ring)
    pairs = [(ring[i], ring[(i + steps) % count]) for i in range(count)]
    return lax.ppermute(value, "expert", pairs)


def expert_rows(inputs, grads, w_gate, w_up):
    gate = jnp.dot(inputs, w_gate, preferred_element_type=jnp.float32)
    upper = jnp.dot(inputs, w_up, preferred_element_type=jnp.float32)
    return gate, upper


def row_grads(inputs, grads, w_gate, w_up, w_down):
    gate, upper = expert_rows(inputs, grads, w_gate, w_up)
    sig = jax.nn.sigmoid(gate)
    act = gate * sig
    hidden = (act * upper).astype(jnp.bfloat16)
    dact = lax.dot_general(
        grads, w_down, (((1,), (1,)), ((), ())), preferred_element_type=jnp.float32
    )
    d_up = (dact * act).astype(jnp.bfloat16)
    d_gate = (dact * upper * sig * (1.0 + gate * (1.0 - sig))).astype(jnp.bfloat16)
    inner = (((1,), (1,)), ((), ()))
    d_in = lax.dot_general(d_gate, w_gate, inner, preferred_element_type=jnp.float32)
    d_in = d_in + lax.dot_general(d_up, w_up, inner, preferred_element_type=jnp.float32)
    return d_in.astype(jnp.bfloat16), hidden, d_gate, d_up


def shards(upstream, layer_input, routes, gate_units, gate_weight, up_weight, down_weight):
    received = passed_along(upstream, "section", -1)[0]
    tokens = layer_input[0]
    tok_rows, width = tokens.shape
    count = lax.axis_size("expert")
    experts = count // 2
    expert = lax.axis_index("expert") // 2
    ring = ring_order(count)
    lanes = 128
    units = gate_units[0].astype(jnp.float32) / 256.0
    chosen = routes[0][:, :, None] == jnp.arange(lanes, dtype=jnp.int32)[None, None, :]
    gains = jnp.sum(jnp.where(chosen, units[:, :, None], 0.0), axis=1).astype(jnp.bfloat16)
    packed = jnp.concatenate([tokens, received, gains], axis=1)
    early = jnp.concatenate([tokens, gains], axis=1)
    rows = tok_rows // 2
    w_gate, w_up, w_down = gate_weight[0], up_weight[0], down_weight[0]
    pick = (jnp.arange(lanes, dtype=jnp.int32) == expert).astype(jnp.float32)

    data = packed.shape[1]

    def contribution(block):
        inputs = block[:, :width]
        grads = block[:, width : 2 * width].astype(jnp.float32)
        gain = jnp.sum(block[:, 2 * width : data].astype(jnp.float32) * pick[None, :], axis=1)
        weighted = (gain[:, None] * grads).astype(jnp.bfloat16)
        part, hidden, d_gate, d_up = row_grads(inputs, weighted, w_gate, w_up, w_down)
        kept.append((inputs, weighted, hidden, d_gate, d_up))
        return part[:rows], part[rows:]

    def added(trail, part):
        return (trail.astype(jnp.float32) + part.astype(jnp.float32)).astype(jnp.bfloat16)

    kept = []
    ahead, behind = packed[:rows], packed[rows:]
    early_ahead = along_ring(early[:rows], ring, 1)
    early_behind = along_ring(early[rows:], ring, -1)
    late_ahead = along_ring(received[:rows], ring, 1)
    late_behind = along_ring(received[rows:], ring, -1)
    parts = contribution(packed)
    for step in range(1, count):
        if step == 1:
            ahead, behind = (
                jnp.concatenate([e[:, :width], l, e[:, width:]], axis=1)
                for e, l in ((early_ahead, late_ahead), (early_behind, late_behind))
            )
        else:
            ahead, behind = sent_ahead, sent_behind
        if step == 1:
            sums = parts
        else:
            trail = (ahead[:, data:], behind[:, data:])
            sums = (added(trail[0], parts[0]), added(trail[1], parts[1]))
        if step < count - 1:
            outgoing = (
                jnp.concatenate([ahead[:, :data], sums[0]], axis=1),
                jnp.concatenate([behind[:, :data], sums[1]], axis=1),
            )
        else:
            outgoing = sums
        block = jnp.concatenate([ahead[:, :data], behind[:, :data]], axis=0)
        outgoing, block = lax.optimization_barrier((outgoing, block))
        sent_ahead = along_ring(outgoing[0], ring, 1)
        sent_behind = along_ring(outgoing[1], ring, -1)
        parts = contribution(block)
    trail = (sent_ahead, sent_behind)
    sums = (added(trail[0], parts[0]), added(trail[1], parts[1]))
    total = jnp.concatenate([along_ring(sums[0], ring, 1), along_ring(sums[1], ring, -1)], axis=0)
    outer = (((0,), (0,)), ((), ()))
    acc = None
    for first, last in ((0, count // 2), (count // 2, count - 1), (count - 1, count)):
        inputs, weighted, hidden, d_gate, d_up = (
            jnp.concatenate([k[i] for k in kept[first:last]], axis=0) for i in range(5)
        )
        grads = (
            lax.dot_general(inputs, d_gate, outer, preferred_element_type=jnp.float32),
            lax.dot_general(inputs, d_up, outer, preferred_element_type=jnp.float32),
            lax.dot_general(hidden, weighted, outer, preferred_element_type=jnp.float32),
        )
        acc = grads if acc is None else tuple(a + g for a, g in zip(acc, grads))
    grad_input = (total.astype(jnp.float32) + received.astype(jnp.float32)).astype(jnp.bfloat16)
    g_gate, g_up, g_down = (a.astype(jnp.bfloat16) for a in acc)
    return (grad_input[None], g_gate[None], g_up[None], g_down[None])


def solution(mesh):
    in_specs = (
        P("section", "expert", None),
        P("section", "expert", None),
        P("section", "expert", None),
        P("section", "expert", None),
        P("section", None, "expert"),
        P("section", None, "expert"),
        P("section", "expert", None),
    )
    out_specs = (
        P("section", "expert", None),
        P("section", None, "expert"),
        P("section", None, "expert"),
        P("section", "expert", None),
    )
    return jax.shard_map(shards, mesh=mesh, in_specs=in_specs, out_specs=out_specs, check_vma=False)
```

```python
import jax
import jax.numpy as jnp
from jax import lax
from jax.sharding import PartitionSpec as P


def passed_along(value, axis, steps):
    count = lax.axis_size(axis)
    pairs = [(source, (source + steps) % count) for source in range(count)]
    return lax.ppermute(value, axis, pairs)


def ring_order(count):
    half = count // 2
    return [2 * a for a in range(half)] + [2 * a + 1 for a in reversed(range(half))]


def along_ring(value, ring, steps):
    count = len(ring)
    pairs = [(ring[i], ring[(i + steps) % count]) for i in range(count)]
    return lax.ppermute(value, "expert", pairs)


def expert_rows(inputs, grads, w_gate, w_up):
    gate = jnp.dot(inputs, w_gate, preferred_element_type=jnp.float32)
    upper = jnp.dot(inputs, w_up, preferred_element_type=jnp.float32)
    return gate, upper


def row_grads(inputs, grads, w_gate, w_up, w_down):
    gate, upper = expert_rows(inputs, grads, w_gate, w_up)
    sig = jax.nn.sigmoid(gate)
    act = gate * sig
    hidden = (act * upper).astype(jnp.bfloat16)
    dact = lax.dot_general(
        grads, w_down, (((1,), (1,)), ((), ())), preferred_element_type=jnp.float32
    )
    d_up = (dact * act).astype(jnp.bfloat16)
    d_gate = (dact * upper * sig * (1.0 + gate * (1.0 - sig))).astype(jnp.bfloat16)
    inner = (((1,), (1,)), ((), ()))
    d_in = lax.dot_general(d_gate, w_gate, inner, preferred_element_type=jnp.float32)
    d_in = d_in + lax.dot_general(d_up, w_up, inner, preferred_element_type=jnp.float32)
    return d_in.astype(jnp.bfloat16), hidden, d_gate, d_up


def shards(upstream, layer_input, routes, gate_units, gate_weight, up_weight, down_weight):
    tokens = layer_input[0]
    tok_rows, width = tokens.shape
    rows = tok_rows // 2
    halves = [passed_along(upstream[0, :rows], "section", -1), passed_along(upstream[0, rows:], "section", -1)]
    received = jnp.concatenate(halves, axis=0)
    count = lax.axis_size("expert")
    experts = count // 2
    expert = lax.axis_index("expert") // 2
    ring = ring_order(count)
    lanes = 128
    units = gate_units[0].astype(jnp.float32) / 256.0
    chosen = routes[0][:, :, None] == jnp.arange(lanes, dtype=jnp.int32)[None, None, :]
    gains = jnp.sum(jnp.where(chosen, units[:, :, None], 0.0), axis=1).astype(jnp.bfloat16)
    packed = jnp.concatenate([tokens, received, gains], axis=1)
    early = jnp.concatenate([tokens, gains], axis=1)
    w_gate, w_up, w_down = gate_weight[0], up_weight[0], down_weight[0]
    pick = (jnp.arange(lanes, dtype=jnp.int32) == expert).astype(jnp.float32)

    data = packed.shape[1]

    def contribution(block):
        inputs = block[:, :width]
        grads = block[:, width : 2 * width].astype(jnp.float32)
        gain = jnp.sum(block[:, 2 * width : data].astype(jnp.float32) * pick[None, :], axis=1)
        weighted = (gain[:, None] * grads).astype(jnp.bfloat16)
        part, hidden, d_gate, d_up = row_grads(inputs, weighted, w_gate, w_up, w_down)
        kept.append((inputs, weighted, hidden, d_gate, d_up))
        return part[:rows], part[rows:]

    def added(trail, part):
        return (trail.astype(jnp.float32) + part.astype(jnp.float32)).astype(jnp.bfloat16)

    kept = []
    ahead, behind = packed[:rows], packed[rows:]
    early_ahead = along_ring(early[:rows], ring, 1)
    early_behind = along_ring(early[rows:], ring, -1)
    late_ahead = along_ring(halves[0], ring, 1)
    late_behind = along_ring(halves[1], ring, -1)
    parts = contribution(packed)
    for step in range(1, count):
        if step == 1:
            ahead, behind = (
                jnp.concatenate([e[:, :width], l, e[:, width:]], axis=1)
                for e, l in ((early_ahead, late_ahead), (early_behind, late_behind))
            )
        else:
            ahead, behind = sent_ahead, sent_behind
        if step == 1:
            sums = parts
        else:
            trail = (ahead[:, data:], behind[:, data:])
            sums = (added(trail[0], parts[0]), added(trail[1], parts[1]))
        if step < count - 1:
            outgoing = (
                jnp.concatenate([ahead[:, :data], sums[0]], axis=1),
                jnp.concatenate([behind[:, :data], sums[1]], axis=1),
            )
        else:
            outgoing = sums
        block = jnp.concatenate([ahead[:, :data], behind[:, :data]], axis=0)
        outgoing, block = lax.optimization_barrier((outgoing, block))
        sent_ahead = along_ring(outgoing[0], ring, 1)
        sent_behind = along_ring(outgoing[1], ring, -1)
        parts = contribution(block)
    trail = (sent_ahead, sent_behind)
    sums = (added(trail[0], parts[0]), added(trail[1], parts[1]))
    total = jnp.concatenate([along_ring(sums[0], ring, 1), along_ring(sums[1], ring, -1)], axis=0)
    outer = (((0,), (0,)), ((), ()))
    acc = None
    for first, last in ((0, count // 2), (count // 2, count - 1), (count - 1, count)):
        inputs, weighted, hidden, d_gate, d_up = (
            jnp.concatenate([k[i] for k in kept[first:last]], axis=0) for i in range(5)
        )
        grads = (
            lax.dot_general(inputs, d_gate, outer, preferred_element_type=jnp.float32),
            lax.dot_general(inputs, d_up, outer, preferred_element_type=jnp.float32),
            lax.dot_general(hidden, weighted, outer, preferred_element_type=jnp.float32),
        )
        acc = grads if acc is None else tuple(a + g for a, g in zip(acc, grads))
    grad_input = (total.astype(jnp.float32) + received.astype(jnp.float32)).astype(jnp.bfloat16)
    g_gate, g_up, g_down = (a.astype(jnp.bfloat16) for a in acc)
    return (grad_input[None], g_gate[None], g_up[None], g_down[None])


def solution(mesh):
    in_specs = (
        P("section", "expert", None),
        P("section", "expert", None),
        P("section", "expert", None),
        P("section", "expert", None),
        P("section", None, "expert"),
        P("section", None, "expert"),
        P("section", "expert", None),
    )
    out_specs = (
        P("section", "expert", None),
        P("section", None, "expert"),
        P("section", None, "expert"),
        P("section", "expert", None),
    )
    return jax.shard_map(shards, mesh=mesh, in_specs=in_specs, out_specs=out_specs, check_vma=False)
```

```python
import jax
import jax.numpy as jnp
from jax import lax
from jax.sharding import PartitionSpec as P


def passed_along(value, axis, steps):
    count = lax.axis_size(axis)
    pairs = [(source, (source + steps) % count) for source in range(count)]
    return lax.ppermute(value, axis, pairs)


def ring_order(count):
    half = count // 2
    return [2 * a for a in range(half)] + [2 * a + 1 for a in reversed(range(half))]


def along_ring(value, ring, steps):
    count = len(ring)
    pairs = [(ring[i], ring[(i + steps) % count]) for i in range(count)]
    return lax.ppermute(value, "expert", pairs)


def diagonal(value, ring, steps):
    count, sections = len(ring), lax.axis_size("section")
    pairs = [
        (((section + 1) % sections) * count + ring[i], section * count + ring[(i + steps) % count])
        for section in range(sections)
        for i in range(count)
    ]
    return lax.ppermute(value, ("section", "expert"), pairs)


def expert_rows(inputs, grads, w_gate, w_up):
    gate = jnp.dot(inputs, w_gate, preferred_element_type=jnp.float32)
    upper = jnp.dot(inputs, w_up, preferred_element_type=jnp.float32)
    return gate, upper


def row_grads(inputs, grads, w_gate, w_up, w_down):
    gate, upper = expert_rows(inputs, grads, w_gate, w_up)
    sig = jax.nn.sigmoid(gate)
    act = gate * sig
    hidden = (act * upper).astype(jnp.bfloat16)
    dact = lax.dot_general(
        grads, w_down, (((1,), (1,)), ((), ())), preferred_element_type=jnp.float32
    )
    d_up = (dact * act).astype(jnp.bfloat16)
    d_gate = (dact * upper * sig * (1.0 + gate * (1.0 - sig))).astype(jnp.bfloat16)
    inner = (((1,), (1,)), ((), ()))
    d_in = lax.dot_general(d_gate, w_gate, inner, preferred_element_type=jnp.float32)
    d_in = d_in + lax.dot_general(d_up, w_up, inner, preferred_element_type=jnp.float32)
    return d_in.astype(jnp.bfloat16), hidden, d_gate, d_up


def shards(upstream, layer_input, routes, gate_units, gate_weight, up_weight, down_weight):
    received = passed_along(upstream, "section", -1)[0]
    tokens = layer_input[0]
    tok_rows, width = tokens.shape
    count = lax.axis_size("expert")
    experts = count // 2
    expert = lax.axis_index("expert") // 2
    ring = ring_order(count)
    lanes = 128
    units = gate_units[0].astype(jnp.float32) / 256.0
    chosen = routes[0][:, :, None] == jnp.arange(lanes, dtype=jnp.int32)[None, None, :]
    gains = jnp.sum(jnp.where(chosen, units[:, :, None], 0.0), axis=1).astype(jnp.bfloat16)
    packed = jnp.concatenate([tokens, received, gains], axis=1)
    early = jnp.concatenate([tokens, gains], axis=1)
    rows = tok_rows // 2
    w_gate, w_up, w_down = gate_weight[0], up_weight[0], down_weight[0]
    pick = (jnp.arange(lanes, dtype=jnp.int32) == expert).astype(jnp.float32)

    data = packed.shape[1]

    def contribution(block):
        inputs = block[:, :width]
        grads = block[:, width : 2 * width].astype(jnp.float32)
        gain = jnp.sum(block[:, 2 * width : data].astype(jnp.float32) * pick[None, :], axis=1)
        weighted = (gain[:, None] * grads).astype(jnp.bfloat16)
        part, hidden, d_gate, d_up = row_grads(inputs, weighted, w_gate, w_up, w_down)
        kept.append((inputs, weighted, hidden, d_gate, d_up))
        return part[:rows], part[rows:]

    def added(trail, part):
        return (trail.astype(jnp.float32) + part.astype(jnp.float32)).astype(jnp.bfloat16)

    kept = []
    ahead, behind = packed[:rows], packed[rows:]
    early_ahead = along_ring(early[:rows], ring, 1)
    early_behind = along_ring(early[rows:], ring, -1)
    late_ahead = diagonal(upstream[0, :rows], ring, 1)
    late_behind = diagonal(upstream[0, rows:], ring, -1)
    parts = contribution(packed)
    for step in range(1, count):
        if step == 1:
            ahead, behind = (
                jnp.concatenate([e[:, :width], l, e[:, width:]], axis=1)
                for e, l in ((early_ahead, late_ahead), (early_behind, late_behind))
            )
        else:
            ahead, behind = sent_ahead, sent_behind
        if step == 1:
            sums = parts
        else:
            trail = (ahead[:, data:], behind[:, data:])
            sums = (added(trail[0], parts[0]), added(trail[1], parts[1]))
        if step < count - 1:
            outgoing = (
                jnp.concatenate([ahead[:, :data], sums[0]], axis=1),
                jnp.concatenate([behind[:, :data], sums[1]], axis=1),
            )
        else:
            outgoing = sums
        block = jnp.concatenate([ahead[:, :data], behind[:, :data]], axis=0)
        outgoing, block = lax.optimization_barrier((outgoing, block))
        sent_ahead = along_ring(outgoing[0], ring, 1)
        sent_behind = along_ring(outgoing[1], ring, -1)
        parts = contribution(block)
    trail = (sent_ahead, sent_behind)
    sums = (added(trail[0], parts[0]), added(trail[1], parts[1]))
    total = jnp.concatenate([along_ring(sums[0], ring, 1), along_ring(sums[1], ring, -1)], axis=0)
    outer = (((0,), (0,)), ((), ()))
    acc = None
    for first, last in ((0, count // 2), (count // 2, count - 1), (count - 1, count)):
        inputs, weighted, hidden, d_gate, d_up = (
            jnp.concatenate([k[i] for k in kept[first:last]], axis=0) for i in range(5)
        )
        grads = (
            lax.dot_general(inputs, d_gate, outer, preferred_element_type=jnp.float32),
            lax.dot_general(inputs, d_up, outer, preferred_element_type=jnp.float32),
            lax.dot_general(hidden, weighted, outer, preferred_element_type=jnp.float32),
        )
        acc = grads if acc is None else tuple(a + g for a, g in zip(acc, grads))
    grad_input = (total.astype(jnp.float32) + received.astype(jnp.float32)).astype(jnp.bfloat16)
    g_gate, g_up, g_down = (a.astype(jnp.bfloat16) for a in acc)
    return (grad_input[None], g_gate[None], g_up[None], g_down[None])


def solution(mesh):
    in_specs = (
        P("section", "expert", None),
        P("section", "expert", None),
        P("section", "expert", None),
        P("section", "expert", None),
        P("section", None, "expert"),
        P("section", None, "expert"),
        P("section", "expert", None),
    )
    out_specs = (
        P("section", "expert", None),
        P("section", None, "expert"),
        P("section", None, "expert"),
        P("section", "expert", None),
    )
    return jax.shard_map(shards, mesh=mesh, in_specs=in_specs, out_specs=out_specs, check_vma=False)
```

```python
import jax
import jax.numpy as jnp
from jax import lax
from jax.sharding import PartitionSpec as P


def passed_along(value, axis, steps):
    count = lax.axis_size(axis)
    pairs = [(source, (source + steps) % count) for source in range(count)]
    return lax.ppermute(value, axis, pairs)


def ring_order(count):
    half = count // 2
    return [2 * a for a in range(half)] + [2 * a + 1 for a in reversed(range(half))]


def along_ring(value, ring, steps):
    count = len(ring)
    pairs = [(ring[i], ring[(i + steps) % count]) for i in range(count)]
    return lax.ppermute(value, "expert", pairs)


def expert_rows(inputs, grads, w_gate, w_up):
    gate = jnp.dot(inputs, w_gate, preferred_element_type=jnp.float32)
    upper = jnp.dot(inputs, w_up, preferred_element_type=jnp.float32)
    return gate, upper


def row_grads(inputs, grads, w_gate, w_up, w_down):
    gate, upper = expert_rows(inputs, grads, w_gate, w_up)
    sig = jax.nn.sigmoid(gate)
    act = gate * sig
    hidden = (act * upper).astype(jnp.bfloat16)
    dact = lax.dot_general(
        grads, w_down, (((1,), (1,)), ((), ())), preferred_element_type=jnp.float32
    )
    d_up = (dact * act).astype(jnp.bfloat16)
    d_gate = (dact * upper * sig * (1.0 + gate * (1.0 - sig))).astype(jnp.bfloat16)
    inner = (((1,), (1,)), ((), ()))
    d_in = lax.dot_general(d_gate, w_gate, inner, preferred_element_type=jnp.float32)
    d_in = d_in + lax.dot_general(d_up, w_up, inner, preferred_element_type=jnp.float32)
    return d_in.astype(jnp.bfloat16), hidden, d_gate, d_up


def shards(upstream, layer_input, routes, gate_units, gate_weight, up_weight, down_weight):
    received = passed_along(upstream, "section", -1)[0]
    tokens = layer_input[0]
    tok_rows, width = tokens.shape
    count = lax.axis_size("expert")
    experts = count // 2
    expert = lax.axis_index("expert") // 2
    ring = ring_order(count)
    lanes = 128
    units = gate_units[0].astype(jnp.float32) / 256.0
    chosen = routes[0][:, :, None] == jnp.arange(lanes, dtype=jnp.int32)[None, None, :]
    gains = jnp.sum(jnp.where(chosen, units[:, :, None], 0.0), axis=1).astype(jnp.bfloat16)
    packed = jnp.concatenate([tokens, received, gains], axis=1)
    early = jnp.concatenate([tokens, gains], axis=1)
    early, received = lax.optimization_barrier((early, received))
    rows = tok_rows // 2
    w_gate, w_up, w_down = gate_weight[0], up_weight[0], down_weight[0]
    pick = (jnp.arange(lanes, dtype=jnp.int32) == expert).astype(jnp.float32)

    data = packed.shape[1]

    def contribution(block):
        inputs = block[:, :width]
        grads = block[:, width : 2 * width].astype(jnp.float32)
        gain = jnp.sum(block[:, 2 * width : data].astype(jnp.float32) * pick[None, :], axis=1)
        weighted = (gain[:, None] * grads).astype(jnp.bfloat16)
        part, hidden, d_gate, d_up = row_grads(inputs, weighted, w_gate, w_up, w_down)
        kept.append((inputs, weighted, hidden, d_gate, d_up))
        return part[:rows], part[rows:]

    def added(trail, part):
        return (trail.astype(jnp.float32) + part.astype(jnp.float32)).astype(jnp.bfloat16)

    kept = []
    ahead, behind = packed[:rows], packed[rows:]
    early_ahead = along_ring(early[:rows], ring, 1)
    early_behind = along_ring(early[rows:], ring, -1)
    late_ahead = along_ring(received[:rows], ring, 1)
    late_behind = along_ring(received[rows:], ring, -1)
    parts = contribution(packed)
    for step in range(1, count):
        if step == 1:
            ahead, behind = (
                jnp.concatenate([e[:, :width], l, e[:, width:]], axis=1)
                for e, l in ((early_ahead, late_ahead), (early_behind, late_behind))
            )
        else:
            ahead, behind = sent_ahead, sent_behind
        if step == 1:
            sums = parts
        else:
            trail = (ahead[:, data:], behind[:, data:])
            sums = (added(trail[0], parts[0]), added(trail[1], parts[1]))
        if step < count - 1:
            outgoing = (
                jnp.concatenate([ahead[:, :data], sums[0]], axis=1),
                jnp.concatenate([behind[:, :data], sums[1]], axis=1),
            )
        else:
            outgoing = sums
        block = jnp.concatenate([ahead[:, :data], behind[:, :data]], axis=0)
        outgoing, block = lax.optimization_barrier((outgoing, block))
        sent_ahead = along_ring(outgoing[0], ring, 1)
        sent_behind = along_ring(outgoing[1], ring, -1)
        parts = contribution(block)
    trail = (sent_ahead, sent_behind)
    sums = (added(trail[0], parts[0]), added(trail[1], parts[1]))
    total = jnp.concatenate([along_ring(sums[0], ring, 1), along_ring(sums[1], ring, -1)], axis=0)
    outer = (((0,), (0,)), ((), ()))
    acc = None
    for first, last in ((0, count // 2), (count // 2, count - 1), (count - 1, count)):
        inputs, weighted, hidden, d_gate, d_up = (
            jnp.concatenate([k[i] for k in kept[first:last]], axis=0) for i in range(5)
        )
        grads = (
            lax.dot_general(inputs, d_gate, outer, preferred_element_type=jnp.float32),
            lax.dot_general(inputs, d_up, outer, preferred_element_type=jnp.float32),
            lax.dot_general(hidden, weighted, outer, preferred_element_type=jnp.float32),
        )
        acc = grads if acc is None else tuple(a + g for a, g in zip(acc, grads))
    grad_input = (total.astype(jnp.float32) + received.astype(jnp.float32)).astype(jnp.bfloat16)
    g_gate, g_up, g_down = (a.astype(jnp.bfloat16) for a in acc)
    return (grad_input[None], g_gate[None], g_up[None], g_down[None])


def solution(mesh):
    in_specs = (
        P("section", "expert", None),
        P("section", "expert", None),
        P("section", "expert", None),
        P("section", "expert", None),
        P("section", None, "expert"),
        P("section", None, "expert"),
        P("section", "expert", None),
    )
    out_specs = (
        P("section", "expert", None),
        P("section", None, "expert"),
        P("section", None, "expert"),
        P("section", "expert", None),
    )
    return jax.shard_map(shards, mesh=mesh, in_specs=in_specs, out_specs=out_specs, check_vma=False)
```

```python
import jax
import jax.numpy as jnp
from jax import lax
from jax.sharding import PartitionSpec as P


def passed_along(value, axis, steps):
    count = lax.axis_size(axis)
    pairs = [(source, (source + steps) % count) for source in range(count)]
    return lax.ppermute(value, axis, pairs)


def ring_order(count):
    half = count // 2
    return [2 * a for a in range(half)] + [2 * a + 1 for a in reversed(range(half))]


def along_ring(value, ring, steps):
    count = len(ring)
    pairs = [(ring[i], ring[(i + steps) % count]) for i in range(count)]
    return lax.ppermute(value, "expert", pairs)


def expert_rows(inputs, grads, w_gate, w_up):
    gate = jnp.dot(inputs, w_gate, preferred_element_type=jnp.float32)
    upper = jnp.dot(inputs, w_up, preferred_element_type=jnp.float32)
    return gate, upper


def row_grads(inputs, grads, w_gate, w_up, w_down):
    gate, upper = expert_rows(inputs, grads, w_gate, w_up)
    sig = jax.nn.sigmoid(gate)
    act = gate * sig
    hidden = (act * upper).astype(jnp.bfloat16)
    dact = lax.dot_general(
        grads, w_down, (((1,), (1,)), ((), ())), preferred_element_type=jnp.float32
    )
    d_up = (dact * act).astype(jnp.bfloat16)
    d_gate = (dact * upper * sig * (1.0 + gate * (1.0 - sig))).astype(jnp.bfloat16)
    inner = (((1,), (1,)), ((), ()))
    d_in = lax.dot_general(d_gate, w_gate, inner, preferred_element_type=jnp.float32)
    d_in = d_in + lax.dot_general(d_up, w_up, inner, preferred_element_type=jnp.float32)
    return d_in.astype(jnp.bfloat16), hidden, d_gate, d_up


def shards(upstream, layer_input, routes, gate_units, gate_weight, up_weight, down_weight):
    received = passed_along(upstream, "section", -1)[0]
    tokens = layer_input[0]
    tok_rows, width = tokens.shape
    count = lax.axis_size("expert")
    experts = count // 2
    expert = lax.axis_index("expert") // 2
    ring = ring_order(count)
    lanes = 128
    units = gate_units[0].astype(jnp.float32) / 256.0
    chosen = routes[0][:, :, None] == jnp.arange(lanes, dtype=jnp.int32)[None, None, :]
    gains = jnp.sum(jnp.where(chosen, units[:, :, None], 0.0), axis=1).astype(jnp.bfloat16)
    packed = jnp.concatenate([tokens, received, gains], axis=1)
    early = jnp.concatenate([tokens, gains], axis=1)
    rows = tok_rows // 2
    w_gate, w_up, w_down = gate_weight[0], up_weight[0], down_weight[0]
    pick = (jnp.arange(lanes, dtype=jnp.int32) == expert).astype(jnp.float32)

    data = packed.shape[1]

    def contribution(block):
        inputs = block[:, :width]
        grads = block[:, width : 2 * width].astype(jnp.float32)
        gain = jnp.sum(block[:, 2 * width : data].astype(jnp.float32) * pick[None, :], axis=1)
        weighted = (gain[:, None] * grads).astype(jnp.bfloat16)
        part, hidden, d_gate, d_up = row_grads(inputs, weighted, w_gate, w_up, w_down)
        kept.append((inputs, weighted, hidden, d_gate, d_up))
        return part[:rows], part[rows:]

    def added(trail, part):
        return (trail.astype(jnp.float32) + part.astype(jnp.float32)).astype(jnp.bfloat16)

    kept = []
    ahead, behind = packed[:rows], packed[rows:]
    early_ahead = along_ring(early[:rows], ring, 1)
    early_behind = along_ring(early[rows:], ring, -1)
    late_ahead = along_ring(received[:rows], ring, 1)
    late_behind = along_ring(received[rows:], ring, -1)
    own = contribution(packed)
    parts = None
    for step in range(1, count):
        if step == 1:
            ahead, behind = (
                jnp.concatenate([e[:, :width], l, e[:, width:]], axis=1)
                for e, l in ((early_ahead, late_ahead), (early_behind, late_behind))
            )
        else:
            ahead, behind = sent_ahead, sent_behind
        if step == 1:
            sums = None
        elif step == 2:
            sums = parts
        else:
            trail = (ahead[:, data:], behind[:, data:])
            sums = (added(trail[0], parts[0]), added(trail[1], parts[1]))
        if sums is None:
            outgoing = (ahead[:, :data], behind[:, :data])
        elif step < count - 1:
            outgoing = (
                jnp.concatenate([ahead[:, :data], sums[0]], axis=1),
                jnp.concatenate([behind[:, :data], sums[1]], axis=1),
            )
        else:
            outgoing = sums
        block = jnp.concatenate([ahead[:, :data], behind[:, :data]], axis=0)
        outgoing, block = lax.optimization_barrier((outgoing, block))
        sent_ahead = along_ring(outgoing[0], ring, 1)
        sent_behind = along_ring(outgoing[1], ring, -1)
        parts = contribution(block)
    trail = (sent_ahead, sent_behind)
    sums = (added(trail[0], parts[0]), added(trail[1], parts[1]))
    total = jnp.concatenate([along_ring(sums[0], ring, 1), along_ring(sums[1], ring, -1)], axis=0)
    total = total.astype(jnp.float32) + jnp.concatenate(own, axis=0).astype(jnp.float32)
    outer = (((0,), (0,)), ((), ()))
    acc = None
    for first, last in ((0, count // 2), (count // 2, count - 1), (count - 1, count)):
        inputs, weighted, hidden, d_gate, d_up = (
            jnp.concatenate([k[i] for k in kept[first:last]], axis=0) for i in range(5)
        )
        grads = (
            lax.dot_general(inputs, d_gate, outer, preferred_element_type=jnp.float32),
            lax.dot_general(inputs, d_up, outer, preferred_element_type=jnp.float32),
            lax.dot_general(hidden, weighted, outer, preferred_element_type=jnp.float32),
        )
        acc = grads if acc is None else tuple(a + g for a, g in zip(acc, grads))
    grad_input = (total.astype(jnp.float32) + received.astype(jnp.float32)).astype(jnp.bfloat16)
    g_gate, g_up, g_down = (a.astype(jnp.bfloat16) for a in acc)
    return (grad_input[None], g_gate[None], g_up[None], g_down[None])


def solution(mesh):
    in_specs = (
        P("section", "expert", None),
        P("section", "expert", None),
        P("section", "expert", None),
        P("section", "expert", None),
        P("section", None, "expert"),
        P("section", None, "expert"),
        P("section", "expert", None),
    )
    out_specs = (
        P("section", "expert", None),
        P("section", None, "expert"),
        P("section", None, "expert"),
        P("section", "expert", None),
    )
    return jax.shard_map(shards, mesh=mesh, in_specs=in_specs, out_specs=out_specs, check_vma=False)
```

```python
import jax
import jax.numpy as jnp
from jax import lax
from jax.sharding import PartitionSpec as P


def passed_along(value, axis, steps):
    count = lax.axis_size(axis)
    pairs = [(source, (source + steps) % count) for source in range(count)]
    return lax.ppermute(value, axis, pairs)


def ring_order(count):
    half = count // 2
    return [2 * a for a in range(half)] + [2 * a + 1 for a in reversed(range(half))]


def along_ring(value, ring, steps):
    count = len(ring)
    pairs = [(ring[i], ring[(i + steps) % count]) for i in range(count)]
    return lax.ppermute(value, "expert", pairs)


def diagonal(value, ring, steps):
    count, sections = len(ring), lax.axis_size("section")
    pairs = [
        (((section + 1) % sections) * count + ring[i], section * count + ring[(i + steps) % count])
        for section in range(sections)
        for i in range(count)
    ]
    return lax.ppermute(value, ("section", "expert"), pairs)


def expert_rows(inputs, grads, w_gate, w_up):
    gate = jnp.dot(inputs, w_gate, preferred_element_type=jnp.float32)
    upper = jnp.dot(inputs, w_up, preferred_element_type=jnp.float32)
    return gate, upper


def row_grads(inputs, grads, w_gate, w_up, w_down):
    gate, upper = expert_rows(inputs, grads, w_gate, w_up)
    sig = jax.nn.sigmoid(gate)
    act = gate * sig
    hidden = (act * upper).astype(jnp.bfloat16)
    dact = lax.dot_general(
        grads, w_down, (((1,), (1,)), ((), ())), preferred_element_type=jnp.float32
    )
    d_up = (dact * act).astype(jnp.bfloat16)
    d_gate = (dact * upper * sig * (1.0 + gate * (1.0 - sig))).astype(jnp.bfloat16)
    inner = (((1,), (1,)), ((), ()))
    d_in = lax.dot_general(d_gate, w_gate, inner, preferred_element_type=jnp.float32)
    d_in = d_in + lax.dot_general(d_up, w_up, inner, preferred_element_type=jnp.float32)
    return d_in.astype(jnp.bfloat16), hidden, d_gate, d_up


def shards(upstream, layer_input, routes, gate_units, gate_weight, up_weight, down_weight):
    received = passed_along(upstream, "section", -1)[0]
    tokens = layer_input[0]
    tok_rows, width = tokens.shape
    count = lax.axis_size("expert")
    experts = count // 2
    expert = lax.axis_index("expert") // 2
    ring = ring_order(count)
    lanes = 128
    units = gate_units[0].astype(jnp.float32) / 256.0
    chosen = routes[0][:, :, None] == jnp.arange(lanes, dtype=jnp.int32)[None, None, :]
    gains = jnp.sum(jnp.where(chosen, units[:, :, None], 0.0), axis=1).astype(jnp.bfloat16)
    packed = jnp.concatenate([tokens, received, gains], axis=1)
    early = jnp.concatenate([tokens, gains], axis=1)
    rows = tok_rows // 2
    w_gate, w_up, w_down = gate_weight[0], up_weight[0], down_weight[0]
    pick = (jnp.arange(lanes, dtype=jnp.int32) == expert).astype(jnp.float32)

    data = packed.shape[1]

    def contribution(block):
        inputs = block[:, :width]
        grads = block[:, width : 2 * width].astype(jnp.float32)
        gain = jnp.sum(block[:, 2 * width : data].astype(jnp.float32) * pick[None, :], axis=1)
        weighted = (gain[:, None] * grads).astype(jnp.bfloat16)
        part, hidden, d_gate, d_up = row_grads(inputs, weighted, w_gate, w_up, w_down)
        kept.append((inputs, weighted, hidden, d_gate, d_up))
        return part[:rows], part[rows:]

    def added(trail, part):
        return (trail.astype(jnp.float32) + part.astype(jnp.float32)).astype(jnp.bfloat16)

    kept = []
    ahead, behind = packed[:rows], packed[rows:]
    early_ahead = along_ring(early[:rows], ring, 1)
    early_behind = along_ring(early[rows:], ring, -1)
    late_ahead = diagonal(upstream[0, :rows], ring, 1)
    late_behind = diagonal(upstream[0, rows:], ring, -1)
    own = contribution(packed)
    parts = None
    for step in range(1, count):
        if step == 1:
            ahead, behind = (
                jnp.concatenate([e[:, :width], l, e[:, width:]], axis=1)
                for e, l in ((early_ahead, late_ahead), (early_behind, late_behind))
            )
        else:
            ahead, behind = sent_ahead, sent_behind
        if step == 1:
            sums = None
        elif step == 2:
            sums = parts
        else:
            trail = (ahead[:, data:], behind[:, data:])
            sums = (added(trail[0], parts[0]), added(trail[1], parts[1]))
        if sums is None:
            outgoing = (ahead[:, :data], behind[:, :data])
        elif step < count - 1:
            outgoing = (
                jnp.concatenate([ahead[:, :data], sums[0]], axis=1),
                jnp.concatenate([behind[:, :data], sums[1]], axis=1),
            )
        else:
            outgoing = sums
        block = jnp.concatenate([ahead[:, :data], behind[:, :data]], axis=0)
        outgoing, block = lax.optimization_barrier((outgoing, block))
        sent_ahead = along_ring(outgoing[0], ring, 1)
        sent_behind = along_ring(outgoing[1], ring, -1)
        parts = contribution(block)
    trail = (sent_ahead, sent_behind)
    sums = (added(trail[0], parts[0]), added(trail[1], parts[1]))
    total = jnp.concatenate([along_ring(sums[0], ring, 1), along_ring(sums[1], ring, -1)], axis=0)
    total = total.astype(jnp.float32) + jnp.concatenate(own, axis=0).astype(jnp.float32)
    outer = (((0,), (0,)), ((), ()))
    acc = None
    for first, last in ((0, count // 2), (count // 2, count - 1), (count - 1, count)):
        inputs, weighted, hidden, d_gate, d_up = (
            jnp.concatenate([k[i] for k in kept[first:last]], axis=0) for i in range(5)
        )
        grads = (
            lax.dot_general(inputs, d_gate, outer, preferred_element_type=jnp.float32),
            lax.dot_general(inputs, d_up, outer, preferred_element_type=jnp.float32),
            lax.dot_general(hidden, weighted, outer, preferred_element_type=jnp.float32),
        )
        acc = grads if acc is None else tuple(a + g for a, g in zip(acc, grads))
    grad_input = (total.astype(jnp.float32) + received.astype(jnp.float32)).astype(jnp.bfloat16)
    g_gate, g_up, g_down = (a.astype(jnp.bfloat16) for a in acc)
    return (grad_input[None], g_gate[None], g_up[None], g_down[None])


def solution(mesh):
    in_specs = (
        P("section", "expert", None),
        P("section", "expert", None),
        P("section", "expert", None),
        P("section", "expert", None),
        P("section", None, "expert"),
        P("section", None, "expert"),
        P("section", "expert", None),
    )
    out_specs = (
        P("section", "expert", None),
        P("section", None, "expert"),
        P("section", None, "expert"),
        P("section", "expert", None),
    )
    return jax.shard_map(shards, mesh=mesh, in_specs=in_specs, out_specs=out_specs, check_vma=False)
```

```python
import jax
import jax.numpy as jnp
from jax import lax
from jax.sharding import PartitionSpec as P


def passed_along(value, axis, steps):
    count = lax.axis_size(axis)
    pairs = [(source, (source + steps) % count) for source in range(count)]
    return lax.ppermute(value, axis, pairs)


def ring_order(count):
    half = count // 2
    return [2 * a for a in range(half)] + [2 * a + 1 for a in reversed(range(half))]


def along_ring(value, ring, steps):
    count = len(ring)
    pairs = [(ring[i], ring[(i + steps) % count]) for i in range(count)]
    return lax.ppermute(value, "expert", pairs)


def expert_rows(inputs, grads, w_gate, w_up):
    gate = jnp.dot(inputs, w_gate, preferred_element_type=jnp.float32)
    upper = jnp.dot(inputs, w_up, preferred_element_type=jnp.float32)
    return gate, upper


def row_grads(inputs, grads, w_gate, w_up, w_down):
    gate, upper = expert_rows(inputs, grads, w_gate, w_up)
    sig = jax.nn.sigmoid(gate)
    act = gate * sig
    hidden = (act * upper).astype(jnp.bfloat16)
    dact = lax.dot_general(
        grads, w_down, (((1,), (1,)), ((), ())), preferred_element_type=jnp.float32
    )
    d_up = (dact * act).astype(jnp.bfloat16)
    d_gate = (dact * upper * sig * (1.0 + gate * (1.0 - sig))).astype(jnp.bfloat16)
    inner = (((1,), (1,)), ((), ()))
    d_in = lax.dot_general(d_gate, w_gate, inner, preferred_element_type=jnp.float32)
    d_in = d_in + lax.dot_general(d_up, w_up, inner, preferred_element_type=jnp.float32)
    return d_in.astype(jnp.bfloat16), hidden, d_gate, d_up


def shards(upstream, layer_input, routes, gate_units, gate_weight, up_weight, down_weight):
    received = passed_along(upstream, "section", -1)[0]
    tokens = layer_input[0]
    tok_rows, width = tokens.shape
    count = lax.axis_size("expert")
    experts = count // 2
    expert = lax.axis_index("expert") // 2
    ring = ring_order(count)
    lanes = 128
    units = gate_units[0].astype(jnp.float32) / 256.0
    chosen = routes[0][:, :, None] == jnp.arange(lanes, dtype=jnp.int32)[None, None, :]
    gains = jnp.sum(jnp.where(chosen, units[:, :, None], 0.0), axis=1).astype(jnp.bfloat16)
    packed = jnp.concatenate([tokens, received, gains], axis=1)
    early = jnp.concatenate([tokens, gains], axis=1)
    rows = tok_rows // 2
    w_gate, w_up, w_down = gate_weight[0], up_weight[0], down_weight[0]
    pick = (jnp.arange(lanes, dtype=jnp.int32) == expert).astype(jnp.float32)

    data = packed.shape[1]

    def contribution(block):
        inputs = block[:, :width]
        grads = block[:, width : 2 * width].astype(jnp.float32)
        gain = jnp.sum(block[:, 2 * width : data].astype(jnp.float32) * pick[None, :], axis=1)
        weighted = (gain[:, None] * grads).astype(jnp.bfloat16)
        part, hidden, d_gate, d_up = row_grads(inputs, weighted, w_gate, w_up, w_down)
        kept.append((inputs, weighted, hidden, d_gate, d_up))
        return part[:rows], part[rows:]

    def added(trail, part):
        return (trail.astype(jnp.float32) + part.astype(jnp.float32)).astype(jnp.bfloat16)

    kept = []
    ahead, behind = packed[:rows], packed[rows:]
    early_ahead = along_ring(early[:rows], ring, 1)
    early_behind = along_ring(early[rows:], ring, -1)
    late_ahead = along_ring(received[:rows], ring, 1)
    late_behind = along_ring(received[rows:], ring, -1)
    own = contribution(packed)
    parts = None
    for step in range(1, count):
        if step == 1:
            ahead, behind = (
                jnp.concatenate([e[:, :width], l, e[:, width:]], axis=1)
                for e, l in ((early_ahead, late_ahead), (early_behind, late_behind))
            )
        else:
            ahead, behind = sent_ahead, sent_behind
        if step == 1:
            sums = None
        elif step == 2:
            sums = parts
        else:
            trail = (ahead[:, data:], behind[:, data:])
            sums = (added(trail[0], parts[0]), added(trail[1], parts[1]))
        if sums is None:
            outgoing = (ahead[:, :data], behind[:, :data])
        elif step < count - 1:
            outgoing = (
                jnp.concatenate([ahead[:, :data], sums[0]], axis=1),
                jnp.concatenate([behind[:, :data], sums[1]], axis=1),
            )
        else:
            outgoing = sums
        block = jnp.concatenate([ahead[:, :data], behind[:, :data]], axis=0)
        outgoing, block = lax.optimization_barrier((outgoing, block))
        sent_ahead = along_ring(outgoing[0], ring, 1)
        sent_behind = along_ring(outgoing[1], ring, -1)
        parts = contribution(block)
    trail = (sent_ahead, sent_behind)
    sums = (added(trail[0], parts[0]), added(trail[1], parts[1]))
    total = jnp.concatenate([along_ring(sums[0], ring, 1), along_ring(sums[1], ring, -1)], axis=0)
    total = total.astype(jnp.float32) + jnp.concatenate(own, axis=0).astype(jnp.float32)
    outer = (((0,), (0,)), ((), ()))
    acc = None
    for first, last in ((0, count // 2), (count // 2, count)):
        inputs, weighted, hidden, d_gate, d_up = (
            jnp.concatenate([k[i] for k in kept[first:last]], axis=0) for i in range(5)
        )
        grads = (
            lax.dot_general(inputs, d_gate, outer, preferred_element_type=jnp.float32),
            lax.dot_general(inputs, d_up, outer, preferred_element_type=jnp.float32),
            lax.dot_general(hidden, weighted, outer, preferred_element_type=jnp.float32),
        )
        acc = grads if acc is None else tuple(a + g for a, g in zip(acc, grads))
    grad_input = (total.astype(jnp.float32) + received.astype(jnp.float32)).astype(jnp.bfloat16)
    g_gate, g_up, g_down = (a.astype(jnp.bfloat16) for a in acc)
    return (grad_input[None], g_gate[None], g_up[None], g_down[None])


def solution(mesh):
    in_specs = (
        P("section", "expert", None),
        P("section", "expert", None),
        P("section", "expert", None),
        P("section", "expert", None),
        P("section", None, "expert"),
        P("section", None, "expert"),
        P("section", "expert", None),
    )
    out_specs = (
        P("section", "expert", None),
        P("section", None, "expert"),
        P("section", None, "expert"),
        P("section", "expert", None),
    )
    return jax.shard_map(shards, mesh=mesh, in_specs=in_specs, out_specs=out_specs, check_vma=False)
```

```python
import jax
import jax.numpy as jnp
from jax import lax
from jax.sharding import PartitionSpec as P


def passed_along(value, axis, steps):
    count = lax.axis_size(axis)
    pairs = [(source, (source + steps) % count) for source in range(count)]
    return lax.ppermute(value, axis, pairs)


def ring_order(count):
    half = count // 2
    return [2 * a for a in range(half)] + [2 * a + 1 for a in reversed(range(half))]


def along_ring(value, ring, steps):
    count = len(ring)
    pairs = [(ring[i], ring[(i + steps) % count]) for i in range(count)]
    return lax.ppermute(value, "expert", pairs)


def expert_rows(inputs, grads, w_gate, w_up):
    gate = jnp.dot(inputs, w_gate, preferred_element_type=jnp.float32)
    upper = jnp.dot(inputs, w_up, preferred_element_type=jnp.float32)
    return gate, upper


def row_grads(inputs, grads, w_gate, w_up, w_down):
    gate, upper = expert_rows(inputs, grads, w_gate, w_up)
    sig = jax.nn.sigmoid(gate)
    act = gate * sig
    hidden = (act * upper).astype(jnp.bfloat16)
    dact = lax.dot_general(
        grads, w_down, (((1,), (1,)), ((), ())), preferred_element_type=jnp.float32
    )
    d_up = (dact * act).astype(jnp.bfloat16)
    d_gate = (dact * upper * sig * (1.0 + gate * (1.0 - sig))).astype(jnp.bfloat16)
    inner = (((1,), (1,)), ((), ()))
    d_in = lax.dot_general(d_gate, w_gate, inner, preferred_element_type=jnp.float32)
    d_in = d_in + lax.dot_general(d_up, w_up, inner, preferred_element_type=jnp.float32)
    return d_in.astype(jnp.bfloat16), hidden, d_gate, d_up


def shards(upstream, layer_input, routes, gate_units, gate_weight, up_weight, down_weight):
    received = passed_along(upstream, "section", -1)[0]
    tokens = layer_input[0]
    tok_rows, width = tokens.shape
    count = lax.axis_size("expert")
    experts = count // 2
    expert = lax.axis_index("expert") // 2
    ring = ring_order(count)
    lanes = 128
    units = gate_units[0].astype(jnp.float32) / 256.0
    chosen = routes[0][:, :, None] == jnp.arange(lanes, dtype=jnp.int32)[None, None, :]
    gains = jnp.sum(jnp.where(chosen, units[:, :, None], 0.0), axis=1).astype(jnp.bfloat16)
    packed = jnp.concatenate([tokens, received, gains], axis=1)
    early = jnp.concatenate([tokens, gains], axis=1)
    rows = tok_rows // 2
    w_gate, w_up, w_down = gate_weight[0], up_weight[0], down_weight[0]
    pick = (jnp.arange(lanes, dtype=jnp.int32) == expert).astype(jnp.float32)

    data = packed.shape[1]

    def contribution(block):
        inputs = block[:, :width]
        grads = block[:, width : 2 * width].astype(jnp.float32)
        gain = jnp.sum(block[:, 2 * width : data].astype(jnp.float32) * pick[None, :], axis=1)
        weighted = (gain[:, None] * grads).astype(jnp.bfloat16)
        part, hidden, d_gate, d_up = row_grads(inputs, weighted, w_gate, w_up, w_down)
        kept.append((inputs, weighted, hidden, d_gate, d_up))
        return part[:rows], part[rows:]

    def added(trail, part):
        return (trail.astype(jnp.float32) + part.astype(jnp.float32)).astype(jnp.bfloat16)

    kept = []
    ahead, behind = packed[:rows], packed[rows:]
    early_ahead = along_ring(early[:rows], ring, 1)
    early_behind = along_ring(early[rows:], ring, -1)
    late_ahead = along_ring(received[:rows], ring, 1)
    late_behind = along_ring(received[rows:], ring, -1)
    own = contribution(packed)
    parts = None
    for step in range(1, count):
        if step == 1:
            ahead, behind = (
                jnp.concatenate([e[:, :width], l, e[:, width:]], axis=1)
                for e, l in ((early_ahead, late_ahead), (early_behind, late_behind))
            )
        else:
            ahead, behind = sent_ahead, sent_behind
        if step == 1:
            sums = None
        elif step == 2:
            sums = parts
        else:
            trail = (ahead[:, data:], behind[:, data:])
            sums = (added(trail[0], parts[0]), added(trail[1], parts[1]))
        if sums is None:
            outgoing = (ahead[:, :data], behind[:, :data])
        elif step < count - 1:
            outgoing = (
                jnp.concatenate([ahead[:, :data], sums[0]], axis=1),
                jnp.concatenate([behind[:, :data], sums[1]], axis=1),
            )
        else:
            outgoing = sums
        block = jnp.concatenate([ahead[:, :data], behind[:, :data]], axis=0)
        outgoing, block = lax.optimization_barrier((outgoing, block))
        sent_ahead = along_ring(outgoing[0], ring, 1)
        sent_behind = along_ring(outgoing[1], ring, -1)
        parts = contribution(block)
    trail = (sent_ahead, sent_behind)
    sums = (added(trail[0], parts[0]), added(trail[1], parts[1]))
    total = jnp.concatenate([along_ring(sums[0], ring, 1), along_ring(sums[1], ring, -1)], axis=0)
    total = total.astype(jnp.float32) + jnp.concatenate(own, axis=0).astype(jnp.float32)
    outer = (((0,), (0,)), ((), ()))
    acc = None
    for first, last in ((0, count // 2), (count // 2, count - 2), (count - 2, count)):
        inputs, weighted, hidden, d_gate, d_up = (
            jnp.concatenate([k[i] for k in kept[first:last]], axis=0) for i in range(5)
        )
        grads = (
            lax.dot_general(inputs, d_gate, outer, preferred_element_type=jnp.float32),
            lax.dot_general(inputs, d_up, outer, preferred_element_type=jnp.float32),
            lax.dot_general(hidden, weighted, outer, preferred_element_type=jnp.float32),
        )
        acc = grads if acc is None else tuple(a + g for a, g in zip(acc, grads))
    grad_input = (total.astype(jnp.float32) + received.astype(jnp.float32)).astype(jnp.bfloat16)
    g_gate, g_up, g_down = (a.astype(jnp.bfloat16) for a in acc)
    return (grad_input[None], g_gate[None], g_up[None], g_down[None])


def solution(mesh):
    in_specs = (
        P("section", "expert", None),
        P("section", "expert", None),
        P("section", "expert", None),
        P("section", "expert", None),
        P("section", None, "expert"),
        P("section", None, "expert"),
        P("section", "expert", None),
    )
    out_specs = (
        P("section", "expert", None),
        P("section", None, "expert"),
        P("section", None, "expert"),
        P("section", "expert", None),
    )
    return jax.shard_map(shards, mesh=mesh, in_specs=in_specs, out_specs=out_specs, check_vma=False)
```

```python
import jax
import jax.numpy as jnp
from jax import lax
from jax.sharding import PartitionSpec as P


def passed_along(value, axis, steps):
    count = lax.axis_size(axis)
    pairs = [(source, (source + steps) % count) for source in range(count)]
    return lax.ppermute(value, axis, pairs)


def ring_order(count):
    half = count // 2
    return [2 * a for a in range(half)] + [2 * a + 1 for a in reversed(range(half))]


def along_ring(value, ring, steps):
    count = len(ring)
    pairs = [(ring[i], ring[(i + steps) % count]) for i in range(count)]
    return lax.ppermute(value, "expert", pairs)


def expert_rows(inputs, grads, w_gate, w_up):
    gate = jnp.dot(inputs, w_gate, preferred_element_type=jnp.float32)
    upper = jnp.dot(inputs, w_up, preferred_element_type=jnp.float32)
    return gate, upper


def row_grads(inputs, grads, w_gate, w_up, w_down):
    gate, upper = expert_rows(inputs, grads, w_gate, w_up)
    sig = jax.nn.sigmoid(gate)
    act = gate * sig
    hidden = (act * upper).astype(jnp.bfloat16)
    dact = lax.dot_general(
        grads, w_down, (((1,), (1,)), ((), ())), preferred_element_type=jnp.float32
    )
    d_up = (dact * act).astype(jnp.bfloat16)
    d_gate = (dact * upper * sig * (1.0 + gate * (1.0 - sig))).astype(jnp.bfloat16)
    inner = (((1,), (1,)), ((), ()))
    d_in = lax.dot_general(d_gate, w_gate, inner, preferred_element_type=jnp.float32)
    d_in = d_in + lax.dot_general(d_up, w_up, inner, preferred_element_type=jnp.float32)
    return d_in.astype(jnp.bfloat16), hidden, d_gate, d_up


def shards(upstream, layer_input, routes, gate_units, gate_weight, up_weight, down_weight):
    received = passed_along(upstream, "section", -1)[0]
    tokens = layer_input[0]
    tok_rows, width = tokens.shape
    count = lax.axis_size("expert")
    experts = count // 2
    expert = lax.axis_index("expert") // 2
    ring = ring_order(count)
    lanes = 128
    units = gate_units[0].astype(jnp.float32) / 256.0
    chosen = routes[0][:, :, None] == jnp.arange(lanes, dtype=jnp.int32)[None, None, :]
    gains = jnp.sum(jnp.where(chosen, units[:, :, None], 0.0), axis=1).astype(jnp.bfloat16)
    packed = jnp.concatenate([tokens, received, gains], axis=1)
    early = jnp.concatenate([tokens, gains], axis=1)
    rows = tok_rows // 2
    w_gate, w_up, w_down = gate_weight[0], up_weight[0], down_weight[0]
    pick = (jnp.arange(lanes, dtype=jnp.int32) == expert).astype(jnp.float32)

    data = packed.shape[1]

    def contribution(block):
        inputs = block[:, :width]
        grads = block[:, width : 2 * width].astype(jnp.float32)
        gain = jnp.sum(block[:, 2 * width : data].astype(jnp.float32) * pick[None, :], axis=1)
        weighted = (gain[:, None] * grads).astype(jnp.bfloat16)
        part, hidden, d_gate, d_up = row_grads(inputs, weighted, w_gate, w_up, w_down)
        kept.append((inputs, weighted, hidden, d_gate, d_up))
        return part[:rows], part[rows:]

    def added(trail, part):
        return (trail.astype(jnp.float32) + part.astype(jnp.float32)).astype(jnp.bfloat16)

    kept = []
    ahead, behind = packed[:rows], packed[rows:]
    early_ahead = along_ring(early[:rows], ring, 1)
    early_behind = along_ring(early[rows:], ring, -1)
    late_ahead = along_ring(received[:rows], ring, 1)
    late_behind = along_ring(received[rows:], ring, -1)
    own = contribution(packed)
    parts = None
    for step in range(1, count):
        if step == 1:
            ahead, behind = (
                jnp.concatenate([e[:, :width], l, e[:, width:]], axis=1)
                for e, l in ((early_ahead, late_ahead), (early_behind, late_behind))
            )
        else:
            ahead, behind = sent_ahead, sent_behind
        if step == 1:
            sums = None
        elif step == 2:
            sums = parts
        else:
            trail = (ahead[:, data:], behind[:, data:])
            sums = (added(trail[0], parts[0]), added(trail[1], parts[1]))
        if sums is None:
            outgoing = (ahead[:, :data], behind[:, :data])
        elif step < count - 1:
            outgoing = (
                jnp.concatenate([ahead[:, :data], sums[0]], axis=1),
                jnp.concatenate([behind[:, :data], sums[1]], axis=1),
            )
        else:
            outgoing = sums
        block = jnp.concatenate([ahead[:, :data], behind[:, :data]], axis=0)
        outgoing, block = lax.optimization_barrier((outgoing, block))
        sent_ahead = along_ring(outgoing[0], ring, 1)
        sent_behind = along_ring(outgoing[1], ring, -1)
        parts = contribution(block)
    trail = (sent_ahead, sent_behind)
    sums = (added(trail[0], parts[0]), added(trail[1], parts[1]))
    sums, kept[count - 2 :] = lax.optimization_barrier((sums, kept[count - 2 :]))
    total = jnp.concatenate([along_ring(sums[0], ring, 1), along_ring(sums[1], ring, -1)], axis=0)
    total = total.astype(jnp.float32) + jnp.concatenate(own, axis=0).astype(jnp.float32)
    outer = (((0,), (0,)), ((), ()))
    acc = None
    for first, last in ((0, count // 2), (count // 2, count - 2), (count - 2, count)):
        inputs, weighted, hidden, d_gate, d_up = (
            jnp.concatenate([k[i] for k in kept[first:last]], axis=0) for i in range(5)
        )
        grads = (
            lax.dot_general(inputs, d_gate, outer, preferred_element_type=jnp.float32),
            lax.dot_general(inputs, d_up, outer, preferred_element_type=jnp.float32),
            lax.dot_general(hidden, weighted, outer, preferred_element_type=jnp.float32),
        )
        acc = grads if acc is None else tuple(a + g for a, g in zip(acc, grads))
    grad_input = (total.astype(jnp.float32) + received.astype(jnp.float32)).astype(jnp.bfloat16)
    g_gate, g_up, g_down = (a.astype(jnp.bfloat16) for a in acc)
    return (grad_input[None], g_gate[None], g_up[None], g_down[None])


def solution(mesh):
    in_specs = (
        P("section", "expert", None),
        P("section", "expert", None),
        P("section", "expert", None),
        P("section", "expert", None),
        P("section", None, "expert"),
        P("section", None, "expert"),
        P("section", "expert", None),
    )
    out_specs = (
        P("section", "expert", None),
        P("section", None, "expert"),
        P("section", None, "expert"),
        P("section", "expert", None),
    )
    return jax.shard_map(shards, mesh=mesh, in_specs=in_specs, out_specs=out_specs, check_vma=False)
```

```python
import jax
import jax.numpy as jnp
from jax import lax
from jax.sharding import PartitionSpec as P


def passed_along(value, axis, steps):
    count = lax.axis_size(axis)
    pairs = [(source, (source + steps) % count) for source in range(count)]
    return lax.ppermute(value, axis, pairs)


def ring_order(count):
    half = count // 2
    return [2 * a for a in range(half)] + [2 * a + 1 for a in reversed(range(half))]


def along_ring(value, ring, steps):
    count = len(ring)
    pairs = [(ring[i], ring[(i + steps) % count]) for i in range(count)]
    return lax.ppermute(value, "expert", pairs)


def expert_rows(inputs, grads, w_gate, w_up):
    gate = jnp.dot(inputs, w_gate, preferred_element_type=jnp.float32)
    upper = jnp.dot(inputs, w_up, preferred_element_type=jnp.float32)
    return gate, upper


def row_grads(inputs, grads, w_gate, w_up, w_down):
    gate, upper = expert_rows(inputs, grads, w_gate, w_up)
    sig = jax.nn.sigmoid(gate)
    act = gate * sig
    hidden = (act * upper).astype(jnp.bfloat16)
    dact = lax.dot_general(
        grads, w_down, (((1,), (1,)), ((), ())), preferred_element_type=jnp.float32
    )
    d_up = (dact * act).astype(jnp.bfloat16)
    d_gate = (dact * upper * sig * (1.0 + gate * (1.0 - sig))).astype(jnp.bfloat16)
    inner = (((1,), (1,)), ((), ()))
    d_in = lax.dot_general(d_gate, w_gate, inner, preferred_element_type=jnp.float32)
    d_in = d_in + lax.dot_general(d_up, w_up, inner, preferred_element_type=jnp.float32)
    return d_in.astype(jnp.bfloat16), hidden, d_gate, d_up


def shards(upstream, layer_input, routes, gate_units, gate_weight, up_weight, down_weight):
    received = passed_along(upstream, "section", -1)[0]
    tokens = layer_input[0]
    tok_rows, width = tokens.shape
    count = lax.axis_size("expert")
    experts = count // 2
    expert = lax.axis_index("expert") // 2
    ring = ring_order(count)
    lanes = 128
    units = gate_units[0].astype(jnp.float32) / 256.0
    chosen = routes[0][:, :, None] == jnp.arange(lanes, dtype=jnp.int32)[None, None, :]
    gains = jnp.sum(jnp.where(chosen, units[:, :, None], 0.0), axis=1).astype(jnp.bfloat16)
    packed = jnp.concatenate([tokens, received, gains], axis=1)
    rows = tok_rows // 2
    w_gate, w_up, w_down = gate_weight[0], up_weight[0], down_weight[0]
    pick = (jnp.arange(lanes, dtype=jnp.int32) == expert).astype(jnp.float32)

    data = packed.shape[1]

    def contribution(block):
        inputs = block[:, :width]
        grads = block[:, width : 2 * width].astype(jnp.float32)
        gain = jnp.sum(block[:, 2 * width : data].astype(jnp.float32) * pick[None, :], axis=1)
        weighted = (gain[:, None] * grads).astype(jnp.bfloat16)
        part, hidden, d_gate, d_up = row_grads(inputs, weighted, w_gate, w_up, w_down)
        kept.append((inputs, weighted, hidden, d_gate, d_up))
        return part[:rows], part[rows:]

    def added(trail, part):
        return (trail.astype(jnp.float32) + part.astype(jnp.float32)).astype(jnp.bfloat16)

    kept = []
    ahead, behind = packed[:rows], packed[rows:]
    first_ahead = along_ring(packed[:rows], ring, 1)
    first_behind = along_ring(packed[rows:], ring, -1)
    own = contribution(packed)
    parts = None
    for step in range(1, count):
        if step == 1:
            ahead, behind = first_ahead, first_behind
        else:
            ahead, behind = sent_ahead, sent_behind
        if step == 1:
            sums = None
        elif step == 2:
            sums = parts
        else:
            trail = (ahead[:, data:], behind[:, data:])
            sums = (added(trail[0], parts[0]), added(trail[1], parts[1]))
        if sums is None:
            outgoing = (ahead[:, :data], behind[:, :data])
        elif step < count - 1:
            outgoing = (
                jnp.concatenate([ahead[:, :data], sums[0]], axis=1),
                jnp.concatenate([behind[:, :data], sums[1]], axis=1),
            )
        else:
            outgoing = sums
        block = jnp.concatenate([ahead[:, :data], behind[:, :data]], axis=0)
        outgoing, block = lax.optimization_barrier((outgoing, block))
        sent_ahead = along_ring(outgoing[0], ring, 1)
        sent_behind = along_ring(outgoing[1], ring, -1)
        parts = contribution(block)
    trail = (sent_ahead, sent_behind)
    sums = (added(trail[0], parts[0]), added(trail[1], parts[1]))
    total = jnp.concatenate([along_ring(sums[0], ring, 1), along_ring(sums[1], ring, -1)], axis=0)
    total = total.astype(jnp.float32) + jnp.concatenate(own, axis=0).astype(jnp.float32)
    outer = (((0,), (0,)), ((), ()))
    acc = None
    for first, last in ((0, count // 2), (count // 2, count - 2), (count - 2, count)):
        inputs, weighted, hidden, d_gate, d_up = (
            jnp.concatenate([k[i] for k in kept[first:last]], axis=0) for i in range(5)
        )
        grads = (
            lax.dot_general(inputs, d_gate, outer, preferred_element_type=jnp.float32),
            lax.dot_general(inputs, d_up, outer, preferred_element_type=jnp.float32),
            lax.dot_general(hidden, weighted, outer, preferred_element_type=jnp.float32),
        )
        acc = grads if acc is None else tuple(a + g for a, g in zip(acc, grads))
    grad_input = (total.astype(jnp.float32) + received.astype(jnp.float32)).astype(jnp.bfloat16)
    g_gate, g_up, g_down = (a.astype(jnp.bfloat16) for a in acc)
    return (grad_input[None], g_gate[None], g_up[None], g_down[None])


def solution(mesh):
    in_specs = (
        P("section", "expert", None),
        P("section", "expert", None),
        P("section", "expert", None),
        P("section", "expert", None),
        P("section", None, "expert"),
        P("section", None, "expert"),
        P("section", "expert", None),
    )
    out_specs = (
        P("section", "expert", None),
        P("section", None, "expert"),
        P("section", None, "expert"),
        P("section", "expert", None),
    )
    return jax.shard_map(shards, mesh=mesh, in_specs=in_specs, out_specs=out_specs, check_vma=False)
```

```python
import jax
import jax.numpy as jnp
from jax import lax
from jax.sharding import PartitionSpec as P


def passed_along(value, axis, steps):
    count = lax.axis_size(axis)
    pairs = [(source, (source + steps) % count) for source in range(count)]
    return lax.ppermute(value, axis, pairs)


def ring_order(count):
    half = count // 2
    return [2 * a for a in range(half)] + [2 * a + 1 for a in reversed(range(half))]


def along_ring(value, ring, steps):
    count = len(ring)
    pairs = [(ring[i], ring[(i + steps) % count]) for i in range(count)]
    return lax.ppermute(value, "expert", pairs)


def expert_rows(inputs, grads, w_gate, w_up):
    gate = jnp.dot(inputs, w_gate, preferred_element_type=jnp.float32)
    upper = jnp.dot(inputs, w_up, preferred_element_type=jnp.float32)
    return gate, upper


def row_grads(inputs, grads, w_gate, w_up, w_down):
    gate, upper = expert_rows(inputs, grads, w_gate, w_up)
    sig = jax.nn.sigmoid(gate)
    act = gate * sig
    hidden = (act * upper).astype(jnp.bfloat16)
    dact = lax.dot_general(
        grads, w_down, (((1,), (1,)), ((), ())), preferred_element_type=jnp.float32
    )
    d_up = (dact * act).astype(jnp.bfloat16)
    d_gate = (dact * upper * sig * (1.0 + gate * (1.0 - sig))).astype(jnp.bfloat16)
    inner = (((1,), (1,)), ((), ()))
    d_in = lax.dot_general(d_gate, w_gate, inner, preferred_element_type=jnp.float32)
    d_in = d_in + lax.dot_general(d_up, w_up, inner, preferred_element_type=jnp.float32)
    return d_in.astype(jnp.bfloat16), hidden, d_gate, d_up


def shards(upstream, layer_input, routes, gate_units, gate_weight, up_weight, down_weight):
    received = passed_along(upstream, "section", -1)[0]
    tokens = layer_input[0]
    tok_rows, width = tokens.shape
    count = lax.axis_size("expert")
    experts = count // 2
    expert = lax.axis_index("expert") // 2
    ring = ring_order(count)
    lanes = 128
    units = gate_units[0].astype(jnp.float32) / 256.0
    chosen = routes[0][:, :, None] == jnp.arange(lanes, dtype=jnp.int32)[None, None, :]
    gains = jnp.sum(jnp.where(chosen, units[:, :, None], 0.0), axis=1).astype(jnp.bfloat16)
    packed = jnp.concatenate([tokens, received, gains], axis=1)
    early = jnp.concatenate([tokens, gains], axis=1)
    rows = tok_rows // 2
    w_gate, w_up, w_down = gate_weight[0], up_weight[0], down_weight[0]
    pick = (jnp.arange(lanes, dtype=jnp.int32) == expert).astype(jnp.float32)

    data = packed.shape[1]

    def contribution(block):
        inputs = block[:, :width]
        grads = block[:, width : 2 * width].astype(jnp.float32)
        gain = jnp.sum(block[:, 2 * width : data].astype(jnp.float32) * pick[None, :], axis=1)
        weighted = (gain[:, None] * grads).astype(jnp.bfloat16)
        part, hidden, d_gate, d_up = row_grads(inputs, weighted, w_gate, w_up, w_down)
        kept.append((inputs, weighted, hidden, d_gate, d_up))
        return part[:rows], part[rows:]

    def added(trail, part):
        return (trail.astype(jnp.float32) + part.astype(jnp.float32)).astype(jnp.bfloat16)

    kept = []
    ahead, behind = packed[:rows], packed[rows:]
    early_ahead = along_ring(early[:rows], ring, 1)
    early_behind = along_ring(early[rows:], ring, -1)
    late_ahead = along_ring(received[:rows], ring, 1)
    late_behind = along_ring(received[rows:], ring, -1)
    own = contribution(packed)
    parts = None
    for step in range(1, count):
        if step == 1:
            ahead, behind = (
                jnp.concatenate([e[:, :width], l, e[:, width:]], axis=1)
                for e, l in ((early_ahead, late_ahead), (early_behind, late_behind))
            )
        else:
            ahead, behind = sent_ahead, sent_behind
        if step == 1:
            sums = None
        elif step == 2:
            sums = parts
        else:
            trail = (ahead[:, data:], behind[:, data:])
            sums = (added(trail[0], parts[0]), added(trail[1], parts[1]))
        if sums is None:
            outgoing = (ahead[:, :data], behind[:, :data])
        elif step < count - 1:
            outgoing = (
                jnp.concatenate([ahead[:, :data], sums[0]], axis=1),
                jnp.concatenate([behind[:, :data], sums[1]], axis=1),
            )
        else:
            outgoing = sums
        block = jnp.concatenate([ahead[:, :data], behind[:, :data]], axis=0)
        outgoing, block = lax.optimization_barrier((outgoing, block))
        sent_ahead = along_ring(outgoing[0], ring, 1)
        sent_behind = along_ring(outgoing[1], ring, -1)
        parts = contribution(block)
    trail = (sent_ahead, sent_behind)
    sums = (added(trail[0], parts[0]), added(trail[1], parts[1]))
    total = jnp.concatenate([along_ring(sums[0], ring, 1), along_ring(sums[1], ring, -1)], axis=0)
    total = total.astype(jnp.float32) + jnp.concatenate(own, axis=0).astype(jnp.float32)
    outer = (((0,), (0,)), ((), ()))
    acc = None
    for first, last in ((0, count // 2), (count // 2, count - 2), (count - 2, count - 1), (count - 1, count)):
        inputs, weighted, hidden, d_gate, d_up = (
            jnp.concatenate([k[i] for k in kept[first:last]], axis=0) for i in range(5)
        )
        grads = (
            lax.dot_general(inputs, d_gate, outer, preferred_element_type=jnp.float32),
            lax.dot_general(inputs, d_up, outer, preferred_element_type=jnp.float32),
            lax.dot_general(hidden, weighted, outer, preferred_element_type=jnp.float32),
        )
        acc = grads if acc is None else tuple(a + g for a, g in zip(acc, grads))
    grad_input = (total.astype(jnp.float32) + received.astype(jnp.float32)).astype(jnp.bfloat16)
    g_gate, g_up, g_down = (a.astype(jnp.bfloat16) for a in acc)
    return (grad_input[None], g_gate[None], g_up[None], g_down[None])


def solution(mesh):
    in_specs = (
        P("section", "expert", None),
        P("section", "expert", None),
        P("section", "expert", None),
        P("section", "expert", None),
        P("section", None, "expert"),
        P("section", None, "expert"),
        P("section", "expert", None),
    )
    out_specs = (
        P("section", "expert", None),
        P("section", None, "expert"),
        P("section", None, "expert"),
        P("section", "expert", None),
    )
    return jax.shard_map(shards, mesh=mesh, in_specs=in_specs, out_specs=out_specs, check_vma=False)
```

```python
import jax
import jax.numpy as jnp
from jax import lax
from jax.sharding import PartitionSpec as P


def passed_along(value, axis, steps):
    count = lax.axis_size(axis)
    pairs = [(source, (source + steps) % count) for source in range(count)]
    return lax.ppermute(value, axis, pairs)


def ring_order(count):
    half = count // 2
    return [2 * a for a in range(half)] + [2 * a + 1 for a in reversed(range(half))]


def along_ring(value, ring, steps):
    count = len(ring)
    pairs = [(ring[i], ring[(i + steps) % count]) for i in range(count)]
    return lax.ppermute(value, "expert", pairs)


def expert_rows(inputs, grads, w_gate, w_up):
    gate = jnp.dot(inputs, w_gate, preferred_element_type=jnp.float32)
    upper = jnp.dot(inputs, w_up, preferred_element_type=jnp.float32)
    return gate, upper


def row_grads(inputs, grads, w_gate, w_up, w_down):
    gate, upper = expert_rows(inputs, grads, w_gate, w_up)
    sig = jax.nn.sigmoid(gate)
    act = gate * sig
    hidden = (act * upper).astype(jnp.bfloat16)
    dact = lax.dot_general(
        grads, w_down, (((1,), (1,)), ((), ())), preferred_element_type=jnp.float32
    )
    d_up = (dact * act).astype(jnp.bfloat16)
    d_gate = (dact * upper * sig * (1.0 + gate * (1.0 - sig))).astype(jnp.bfloat16)
    inner = (((1,), (1,)), ((), ()))
    d_in = lax.dot_general(d_gate, w_gate, inner, preferred_element_type=jnp.float32)
    d_in = d_in + lax.dot_general(d_up, w_up, inner, preferred_element_type=jnp.float32)
    return d_in.astype(jnp.bfloat16), hidden, d_gate, d_up


def shards(upstream, layer_input, routes, gate_units, gate_weight, up_weight, down_weight):
    received = passed_along(upstream, "section", -1)[0]
    tokens = layer_input[0]
    tok_rows, width = tokens.shape
    count = lax.axis_size("expert")
    experts = count // 2
    expert = lax.axis_index("expert") // 2
    ring = ring_order(count)
    lanes = 128
    units = gate_units[0].astype(jnp.float32) / 256.0
    chosen = routes[0][:, :, None] == jnp.arange(lanes, dtype=jnp.int32)[None, None, :]
    gains = jnp.sum(jnp.where(chosen, units[:, :, None], 0.0), axis=1).astype(jnp.bfloat16)
    packed = jnp.concatenate([tokens, received, gains], axis=1)
    early = jnp.concatenate([tokens, gains], axis=1)
    rows = tok_rows // 2
    w_gate, w_up, w_down = gate_weight[0], up_weight[0], down_weight[0]
    pick = (jnp.arange(lanes, dtype=jnp.int32) == expert).astype(jnp.float32)

    data = packed.shape[1]

    def contribution(block):
        inputs = block[:, :width]
        grads = block[:, width : 2 * width].astype(jnp.float32)
        gain = jnp.sum(block[:, 2 * width : data].astype(jnp.float32) * pick[None, :], axis=1)
        weighted = (gain[:, None] * grads).astype(jnp.bfloat16)
        part, hidden, d_gate, d_up = row_grads(inputs, weighted, w_gate, w_up, w_down)
        kept.append((inputs, weighted, hidden, d_gate, d_up))
        return part[:rows], part[rows:]

    def added(trail, part):
        return (trail.astype(jnp.float32) + part.astype(jnp.float32)).astype(jnp.bfloat16)

    kept = []
    ahead, behind = packed[:rows], packed[rows:]
    early_ahead = along_ring(early[:rows], ring, 1)
    late_ahead = along_ring(received[:rows], ring, 1)
    first_behind = along_ring(packed[rows:], ring, -1)
    own = contribution(packed)
    parts = None
    for step in range(1, count):
        if step == 1:
            ahead = jnp.concatenate(
                [early_ahead[:, :width], late_ahead, early_ahead[:, width:]], axis=1
            )
            behind = first_behind
        else:
            ahead, behind = sent_ahead, sent_behind
        if step == 1:
            sums = None
        elif step == 2:
            sums = parts
        else:
            trail = (ahead[:, data:], behind[:, data:])
            sums = (added(trail[0], parts[0]), added(trail[1], parts[1]))
        if sums is None:
            outgoing = (ahead[:, :data], behind[:, :data])
        elif step < count - 1:
            outgoing = (
                jnp.concatenate([ahead[:, :data], sums[0]], axis=1),
                jnp.concatenate([behind[:, :data], sums[1]], axis=1),
            )
        else:
            outgoing = sums
        block = jnp.concatenate([ahead[:, :data], behind[:, :data]], axis=0)
        outgoing, block = lax.optimization_barrier((outgoing, block))
        sent_ahead = along_ring(outgoing[0], ring, 1)
        sent_behind = along_ring(outgoing[1], ring, -1)
        parts = contribution(block)
    trail = (sent_ahead, sent_behind)
    sums = (added(trail[0], parts[0]), added(trail[1], parts[1]))
    total = jnp.concatenate([along_ring(sums[0], ring, 1), along_ring(sums[1], ring, -1)], axis=0)
    total = total.astype(jnp.float32) + jnp.concatenate(own, axis=0).astype(jnp.float32)
    outer = (((0,), (0,)), ((), ()))
    acc = None
    for first, last in ((0, count // 2), (count // 2, count - 2), (count - 2, count)):
        inputs, weighted, hidden, d_gate, d_up = (
            jnp.concatenate([k[i] for k in kept[first:last]], axis=0) for i in range(5)
        )
        grads = (
            lax.dot_general(inputs, d_gate, outer, preferred_element_type=jnp.float32),
            lax.dot_general(inputs, d_up, outer, preferred_element_type=jnp.float32),
            lax.dot_general(hidden, weighted, outer, preferred_element_type=jnp.float32),
        )
        acc = grads if acc is None else tuple(a + g for a, g in zip(acc, grads))
    grad_input = (total.astype(jnp.float32) + received.astype(jnp.float32)).astype(jnp.bfloat16)
    g_gate, g_up, g_down = (a.astype(jnp.bfloat16) for a in acc)
    return (grad_input[None], g_gate[None], g_up[None], g_down[None])


def solution(mesh):
    in_specs = (
        P("section", "expert", None),
        P("section", "expert", None),
        P("section", "expert", None),
        P("section", "expert", None),
        P("section", None, "expert"),
        P("section", None, "expert"),
        P("section", "expert", None),
    )
    out_specs = (
        P("section", "expert", None),
        P("section", None, "expert"),
        P("section", None, "expert"),
        P("section", "expert", None),
    )
    return jax.shard_map(shards, mesh=mesh, in_specs=in_specs, out_specs=out_specs, check_vma=False)
```

```python
import jax
import jax.numpy as jnp
from jax import lax
from jax.sharding import PartitionSpec as P


def passed_along(value, axis, steps):
    count = lax.axis_size(axis)
    pairs = [(source, (source + steps) % count) for source in range(count)]
    return lax.ppermute(value, axis, pairs)


def ring_order(count):
    half = count // 2
    return [2 * a for a in range(half)] + [2 * a + 1 for a in reversed(range(half))]


def along_ring(value, ring, steps):
    count = len(ring)
    pairs = [(ring[i], ring[(i + steps) % count]) for i in range(count)]
    return lax.ppermute(value, "expert", pairs)


def expert_rows(inputs, grads, w_gate, w_up):
    gate = jnp.dot(inputs, w_gate, preferred_element_type=jnp.float32)
    upper = jnp.dot(inputs, w_up, preferred_element_type=jnp.float32)
    return gate, upper


def row_grads(inputs, grads, w_gate, w_up, w_down):
    gate, upper = expert_rows(inputs, grads, w_gate, w_up)
    sig = jax.nn.sigmoid(gate)
    act = gate * sig
    hidden = (act * upper).astype(jnp.bfloat16)
    dact = lax.dot_general(
        grads, w_down, (((1,), (1,)), ((), ())), preferred_element_type=jnp.float32
    )
    d_up = (dact * act).astype(jnp.bfloat16)
    d_gate = (dact * upper * sig * (1.0 + gate * (1.0 - sig))).astype(jnp.bfloat16)
    inner = (((1,), (1,)), ((), ()))
    d_in = lax.dot_general(d_gate, w_gate, inner, preferred_element_type=jnp.float32)
    d_in = d_in + lax.dot_general(d_up, w_up, inner, preferred_element_type=jnp.float32)
    return d_in.astype(jnp.bfloat16), hidden, d_gate, d_up


def shards(upstream, layer_input, routes, gate_units, gate_weight, up_weight, down_weight):
    received = passed_along(upstream, "section", -1)[0]
    tokens = layer_input[0]
    tok_rows, width = tokens.shape
    count = lax.axis_size("expert")
    experts = count // 2
    expert = lax.axis_index("expert") // 2
    ring = ring_order(count)
    lanes = 128
    units = gate_units[0].astype(jnp.float32) / 256.0
    chosen = routes[0][:, :, None] == jnp.arange(lanes, dtype=jnp.int32)[None, None, :]
    gains = jnp.sum(jnp.where(chosen, units[:, :, None], 0.0), axis=1).astype(jnp.bfloat16)
    packed = jnp.concatenate([tokens, received, gains], axis=1)
    early = jnp.concatenate([tokens, gains], axis=1)
    rows = tok_rows // 2
    w_gate, w_up, w_down = gate_weight[0], up_weight[0], down_weight[0]
    pick = (jnp.arange(lanes, dtype=jnp.int32) == expert).astype(jnp.float32)

    data = packed.shape[1]

    def contribution(block):
        inputs = block[:, :width]
        grads = block[:, width : 2 * width].astype(jnp.float32)
        gain = jnp.sum(block[:, 2 * width : data].astype(jnp.float32) * pick[None, :], axis=1)
        weighted = (gain[:, None] * grads).astype(jnp.bfloat16)
        part, hidden, d_gate, d_up = row_grads(inputs, weighted, w_gate, w_up, w_down)
        kept.append((inputs, weighted, hidden, d_gate, d_up))
        return part[:rows], part[rows:]

    def added(trail, part):
        return (trail.astype(jnp.float32) + part.astype(jnp.float32)).astype(jnp.bfloat16)

    kept = []
    ahead, behind = packed[:rows], packed[rows:]
    early_ahead = along_ring(early[:rows], ring, 1)
    early_behind = along_ring(early[rows:], ring, -1)
    late_ahead = along_ring(received[:rows], ring, 1)
    late_behind = along_ring(received[rows:], ring, -1)
    own = None
    parts = None
    for step in range(1, count):
        if step == 1:
            ahead, behind = (
                jnp.concatenate([e[:, :width], l, e[:, width:]], axis=1)
                for e, l in ((early_ahead, late_ahead), (early_behind, late_behind))
            )
        else:
            ahead, behind = sent_ahead, sent_behind
        if step == 1:
            sums = None
        elif step == 2:
            sums = parts
        else:
            trail = (ahead[:, data:], behind[:, data:])
            sums = (added(trail[0], parts[0]), added(trail[1], parts[1]))
        if sums is None:
            outgoing = (ahead[:, :data], behind[:, :data])
        elif step < count - 1:
            outgoing = (
                jnp.concatenate([ahead[:, :data], sums[0]], axis=1),
                jnp.concatenate([behind[:, :data], sums[1]], axis=1),
            )
        else:
            outgoing = sums
        block = jnp.concatenate([ahead[:, :data], behind[:, :data]], axis=0)
        if step == 3:
            outgoing, block, mine = lax.optimization_barrier((outgoing, block, packed))
            own = contribution(mine)
        else:
            outgoing, block = lax.optimization_barrier((outgoing, block))
        sent_ahead = along_ring(outgoing[0], ring, 1)
        sent_behind = along_ring(outgoing[1], ring, -1)
        parts = contribution(block)
    trail = (sent_ahead, sent_behind)
    sums = (added(trail[0], parts[0]), added(trail[1], parts[1]))
    total = jnp.concatenate([along_ring(sums[0], ring, 1), along_ring(sums[1], ring, -1)], axis=0)
    total = total.astype(jnp.float32) + jnp.concatenate(own, axis=0).astype(jnp.float32)
    outer = (((0,), (0,)), ((), ()))
    acc = None
    for first, last in ((0, count // 2), (count // 2, count - 2), (count - 2, count)):
        inputs, weighted, hidden, d_gate, d_up = (
            jnp.concatenate([k[i] for k in kept[first:last]], axis=0) for i in range(5)
        )
        grads = (
            lax.dot_general(inputs, d_gate, outer, preferred_element_type=jnp.float32),
            lax.dot_general(inputs, d_up, outer, preferred_element_type=jnp.float32),
            lax.dot_general(hidden, weighted, outer, preferred_element_type=jnp.float32),
        )
        acc = grads if acc is None else tuple(a + g for a, g in zip(acc, grads))
    grad_input = (total.astype(jnp.float32) + received.astype(jnp.float32)).astype(jnp.bfloat16)
    g_gate, g_up, g_down = (a.astype(jnp.bfloat16) for a in acc)
    return (grad_input[None], g_gate[None], g_up[None], g_down[None])


def solution(mesh):
    in_specs = (
        P("section", "expert", None),
        P("section", "expert", None),
        P("section", "expert", None),
        P("section", "expert", None),
        P("section", None, "expert"),
        P("section", None, "expert"),
        P("section", "expert", None),
    )
    out_specs = (
        P("section", "expert", None),
        P("section", None, "expert"),
        P("section", None, "expert"),
        P("section", "expert", None),
    )
    return jax.shard_map(shards, mesh=mesh, in_specs=in_specs, out_specs=out_specs, check_vma=False)
```

```python
import jax
import jax.numpy as jnp
from jax import lax
from jax.sharding import PartitionSpec as P


def passed_along(value, axis, steps):
    count = lax.axis_size(axis)
    pairs = [(source, (source + steps) % count) for source in range(count)]
    return lax.ppermute(value, axis, pairs)


def ring_order(count):
    half = count // 2
    return [2 * a for a in range(half)] + [2 * a + 1 for a in reversed(range(half))]


def along_ring(value, ring, steps):
    count = len(ring)
    pairs = [(ring[i], ring[(i + steps) % count]) for i in range(count)]
    return lax.ppermute(value, "expert", pairs)


def expert_rows(inputs, grads, w_gate, w_up):
    gate = jnp.dot(inputs, w_gate, preferred_element_type=jnp.float32)
    upper = jnp.dot(inputs, w_up, preferred_element_type=jnp.float32)
    return gate, upper


def row_grads(inputs, grads, w_gate, w_up, w_down):
    gate, upper = expert_rows(inputs, grads, w_gate, w_up)
    sig = jax.nn.sigmoid(gate)
    act = gate * sig
    hidden = (act * upper).astype(jnp.bfloat16)
    dact = lax.dot_general(
        grads, w_down, (((1,), (1,)), ((), ())), preferred_element_type=jnp.float32
    )
    d_up = (dact * act).astype(jnp.bfloat16)
    d_gate = (dact * upper * sig * (1.0 + gate * (1.0 - sig))).astype(jnp.bfloat16)
    inner = (((1,), (1,)), ((), ()))
    d_in = lax.dot_general(d_gate, w_gate, inner, preferred_element_type=jnp.float32)
    d_in = d_in + lax.dot_general(d_up, w_up, inner, preferred_element_type=jnp.float32)
    return d_in.astype(jnp.bfloat16), hidden, d_gate, d_up


def shards(upstream, layer_input, routes, gate_units, gate_weight, up_weight, down_weight):
    received = passed_along(upstream, "section", -1)[0]
    tokens = layer_input[0]
    tok_rows, width = tokens.shape
    count = lax.axis_size("expert")
    experts = count // 2
    expert = lax.axis_index("expert") // 2
    ring = ring_order(count)
    lanes = 128
    units = gate_units[0].astype(jnp.float32) / 256.0
    chosen = routes[0][:, :, None] == jnp.arange(lanes, dtype=jnp.int32)[None, None, :]
    gains = jnp.sum(jnp.where(chosen, units[:, :, None], 0.0), axis=1).astype(jnp.bfloat16)
    packed = jnp.concatenate([tokens, received, gains], axis=1)
    early = jnp.concatenate([tokens, gains], axis=1)
    rows = tok_rows // 2
    w_gate, w_up, w_down = gate_weight[0], up_weight[0], down_weight[0]
    pick = (jnp.arange(lanes, dtype=jnp.int32) == expert).astype(jnp.float32)

    data = packed.shape[1]

    def contribution(block):
        inputs = block[:, :width]
        grads = block[:, width : 2 * width].astype(jnp.float32)
        gain = jnp.sum(block[:, 2 * width : data].astype(jnp.float32) * pick[None, :], axis=1)
        weighted = (gain[:, None] * grads).astype(jnp.bfloat16)
        part, hidden, d_gate, d_up = row_grads(inputs, weighted, w_gate, w_up, w_down)
        kept.append((inputs, weighted, hidden, d_gate, d_up))
        return part[:rows], part[rows:]

    def added(trail, part):
        return (trail.astype(jnp.float32) + part.astype(jnp.float32)).astype(jnp.bfloat16)

    kept = []
    ahead, behind = packed[:rows], packed[rows:]
    early_ahead = along_ring(early[:rows], ring, 1)
    early_behind = along_ring(early[rows:], ring, -1)
    late_ahead = along_ring(received[:rows], ring, 1)
    late_behind = along_ring(received[rows:], ring, -1)
    own = contribution(packed)
    parts = None
    for step in range(1, count):
        if step == 1:
            ahead, behind = (
                jnp.concatenate([e[:, :width], l, e[:, width:]], axis=1)
                for e, l in ((early_ahead, late_ahead), (early_behind, late_behind))
            )
        else:
            ahead, behind = sent_ahead, sent_behind
        if step == 1:
            sums = None
        elif step == 2:
            sums = parts
        else:
            trail = (ahead[:, data:], behind[:, data:])
            sums = (added(trail[0], parts[0]), added(trail[1], parts[1]))
        if sums is None:
            outgoing = (ahead[:, :data], behind[:, :data])
        elif step < count - 1:
            outgoing = (
                jnp.concatenate([ahead[:, :data], sums[0]], axis=1),
                jnp.concatenate([behind[:, :data], sums[1]], axis=1),
            )
        else:
            outgoing = sums
        block = jnp.concatenate([ahead[:, :data], behind[:, :data]], axis=0)
        if sums is not None:
            outgoing, block = lax.optimization_barrier((outgoing, block))
        sent_ahead = along_ring(outgoing[0], ring, 1)
        sent_behind = along_ring(outgoing[1], ring, -1)
        parts = contribution(block)
    trail = (sent_ahead, sent_behind)
    sums = (added(trail[0], parts[0]), added(trail[1], parts[1]))
    total = jnp.concatenate([along_ring(sums[0], ring, 1), along_ring(sums[1], ring, -1)], axis=0)
    total = total.astype(jnp.float32) + jnp.concatenate(own, axis=0).astype(jnp.float32)
    outer = (((0,), (0,)), ((), ()))
    acc = None
    for first, last in ((0, count // 2), (count // 2, count - 2), (count - 2, count)):
        inputs, weighted, hidden, d_gate, d_up = (
            jnp.concatenate([k[i] for k in kept[first:last]], axis=0) for i in range(5)
        )
        grads = (
            lax.dot_general(inputs, d_gate, outer, preferred_element_type=jnp.float32),
            lax.dot_general(inputs, d_up, outer, preferred_element_type=jnp.float32),
            lax.dot_general(hidden, weighted, outer, preferred_element_type=jnp.float32),
        )
        acc = grads if acc is None else tuple(a + g for a, g in zip(acc, grads))
    grad_input = (total.astype(jnp.float32) + received.astype(jnp.float32)).astype(jnp.bfloat16)
    g_gate, g_up, g_down = (a.astype(jnp.bfloat16) for a in acc)
    return (grad_input[None], g_gate[None], g_up[None], g_down[None])


def solution(mesh):
    in_specs = (
        P("section", "expert", None),
        P("section", "expert", None),
        P("section", "expert", None),
        P("section", "expert", None),
        P("section", None, "expert"),
        P("section", None, "expert"),
        P("section", "expert", None),
    )
    out_specs = (
        P("section", "expert", None),
        P("section", None, "expert"),
        P("section", None, "expert"),
        P("section", "expert", None),
    )
    return jax.shard_map(shards, mesh=mesh, in_specs=in_specs, out_specs=out_specs, check_vma=False)
```

```python
import jax
import jax.numpy as jnp
from jax import lax
from jax.sharding import PartitionSpec as P


def passed_along(value, axis, steps):
    count = lax.axis_size(axis)
    pairs = [(source, (source + steps) % count) for source in range(count)]
    return lax.ppermute(value, axis, pairs)


def ring_order(count):
    half = count // 2
    return [2 * a for a in range(half)] + [2 * a + 1 for a in reversed(range(half))]


def along_ring(value, ring, steps):
    count = len(ring)
    pairs = [(ring[i], ring[(i + steps) % count]) for i in range(count)]
    return lax.ppermute(value, "expert", pairs)


def expert_rows(inputs, grads, w_gate, w_up):
    gate = jnp.dot(inputs, w_gate, preferred_element_type=jnp.float32)
    upper = jnp.dot(inputs, w_up, preferred_element_type=jnp.float32)
    return gate, upper


def row_grads(inputs, grads, w_gate, w_up, w_down):
    gate, upper = expert_rows(inputs, grads, w_gate, w_up)
    sig = jax.nn.sigmoid(gate)
    act = gate * sig
    hidden = (act * upper).astype(jnp.bfloat16)
    dact = lax.dot_general(
        grads, w_down, (((1,), (1,)), ((), ())), preferred_element_type=jnp.float32
    )
    d_up = (dact * act).astype(jnp.bfloat16)
    d_gate = (dact * upper * sig * (1.0 + gate * (1.0 - sig))).astype(jnp.bfloat16)
    inner = (((1,), (1,)), ((), ()))
    d_in = lax.dot_general(d_gate, w_gate, inner, preferred_element_type=jnp.float32)
    d_in = d_in + lax.dot_general(d_up, w_up, inner, preferred_element_type=jnp.float32)
    return d_in.astype(jnp.bfloat16), hidden, d_gate, d_up


def shards(upstream, layer_input, routes, gate_units, gate_weight, up_weight, down_weight):
    received = passed_along(upstream, "section", -1)[0]
    tokens = layer_input[0]
    tok_rows, width = tokens.shape
    count = lax.axis_size("expert")
    experts = count // 2
    expert = lax.axis_index("expert") // 2
    ring = ring_order(count)
    lanes = 128
    units = gate_units[0].astype(jnp.float32) / 256.0
    chosen = routes[0][:, :, None] == jnp.arange(lanes, dtype=jnp.int32)[None, None, :]
    gains = jnp.sum(jnp.where(chosen, units[:, :, None], 0.0), axis=1).astype(jnp.bfloat16)
    packed = jnp.concatenate([tokens, received, gains], axis=1)
    early = jnp.concatenate([tokens, gains], axis=1)
    rows = tok_rows // 2
    w_gate, w_up, w_down = gate_weight[0], up_weight[0], down_weight[0]
    pick = (jnp.arange(lanes, dtype=jnp.int32) == expert).astype(jnp.float32)

    data = packed.shape[1]

    def contribution(block):
        inputs = block[:, :width]
        grads = block[:, width : 2 * width].astype(jnp.float32)
        gain = jnp.sum(block[:, 2 * width : data].astype(jnp.float32) * pick[None, :], axis=1)
        weighted = (gain[:, None] * grads).astype(jnp.bfloat16)
        part, hidden, d_gate, d_up = row_grads(inputs, weighted, w_gate, w_up, w_down)
        kept.append((inputs, weighted, hidden, d_gate, d_up))
        return part[:rows], part[rows:]

    def added(trail, part):
        return (trail.astype(jnp.float32) + part.astype(jnp.float32)).astype(jnp.bfloat16)

    kept = []
    ahead, behind = packed[:rows], packed[rows:]
    early_ahead = along_ring(early[:rows], ring, 1)
    early_behind = along_ring(early[rows:], ring, -1)
    late_ahead = along_ring(received[:rows], ring, 1)
    late_behind = along_ring(received[rows:], ring, -1)
    own = contribution(packed)
    parts = None
    for step in range(1, count):
        if step == 1:
            ahead, behind = (
                jnp.concatenate([e[:, :width], l, e[:, width:]], axis=1)
                for e, l in ((early_ahead, late_ahead), (early_behind, late_behind))
            )
        else:
            ahead, behind = sent_ahead, sent_behind
        if step == 1:
            sums = None
        elif step == 2:
            sums = parts
        else:
            trail = (ahead[:, data:], behind[:, data:])
            sums = (added(trail[0], parts[0]), added(trail[1], parts[1]))
        if sums is None:
            outgoing = (ahead[:, :data], behind[:, :data])
        elif step < count - 1:
            outgoing = (
                jnp.concatenate([ahead[:, :data], sums[0]], axis=1),
                jnp.concatenate([behind[:, :data], sums[1]], axis=1),
            )
        else:
            outgoing = sums
        block = jnp.concatenate([ahead[:, :data], behind[:, :data]], axis=0)
        outgoing, block = lax.optimization_barrier((outgoing, block))
        sent_ahead = along_ring(outgoing[0], ring, 1)
        sent_behind = along_ring(outgoing[1], ring, -1)
        parts = contribution(block)
    trail = (sent_ahead, sent_behind)
    sums = (added(trail[0], parts[0]), added(trail[1], parts[1]))
    total = jnp.concatenate([along_ring(sums[0], ring, 1), along_ring(sums[1], ring, -1)], axis=0)
    total = total.astype(jnp.float32) + jnp.concatenate(own, axis=0).astype(jnp.float32)
    outer = (((0,), (0,)), ((), ()))
    acc = None
    for first, last in ((0, count // 2 - 1), (count // 2 - 1, count - 2), (count - 2, count)):
        inputs, weighted, hidden, d_gate, d_up = (
            jnp.concatenate([k[i] for k in kept[first:last]], axis=0) for i in range(5)
        )
        grads = (
            lax.dot_general(inputs, d_gate, outer, preferred_element_type=jnp.float32),
            lax.dot_general(inputs, d_up, outer, preferred_element_type=jnp.float32),
            lax.dot_general(hidden, weighted, outer, preferred_element_type=jnp.float32),
        )
        acc = grads if acc is None else tuple(a + g for a, g in zip(acc, grads))
    grad_input = (total.astype(jnp.float32) + received.astype(jnp.float32)).astype(jnp.bfloat16)
    g_gate, g_up, g_down = (a.astype(jnp.bfloat16) for a in acc)
    return (grad_input[None], g_gate[None], g_up[None], g_down[None])


def solution(mesh):
    in_specs = (
        P("section", "expert", None),
        P("section", "expert", None),
        P("section", "expert", None),
        P("section", "expert", None),
        P("section", None, "expert"),
        P("section", None, "expert"),
        P("section", "expert", None),
    )
    out_specs = (
        P("section", "expert", None),
        P("section", None, "expert"),
        P("section", None, "expert"),
        P("section", "expert", None),
    )
    return jax.shard_map(shards, mesh=mesh, in_specs=in_specs, out_specs=out_specs, check_vma=False)
```

```python
import jax
import jax.numpy as jnp
from jax import lax
from jax.sharding import PartitionSpec as P


def passed_along(value, axis, steps):
    count = lax.axis_size(axis)
    pairs = [(source, (source + steps) % count) for source in range(count)]
    return lax.ppermute(value, axis, pairs)


def ring_order(count):
    half = count // 2
    return [2 * a for a in range(half)] + [2 * a + 1 for a in reversed(range(half))]


def along_ring(value, ring, steps):
    count = len(ring)
    pairs = [(ring[i], ring[(i + steps) % count]) for i in range(count)]
    return lax.ppermute(value, "expert", pairs)


def expert_rows(inputs, grads, w_gate, w_up):
    gate = jnp.dot(inputs, w_gate, preferred_element_type=jnp.float32)
    upper = jnp.dot(inputs, w_up, preferred_element_type=jnp.float32)
    return gate, upper


def row_grads(inputs, grads, w_gate, w_up, w_down):
    gate, upper = expert_rows(inputs, grads, w_gate, w_up)
    sig = jax.nn.sigmoid(gate)
    act = gate * sig
    hidden = (act * upper).astype(jnp.bfloat16)
    dact = lax.dot_general(
        grads, w_down, (((1,), (1,)), ((), ())), preferred_element_type=jnp.float32
    )
    d_up = (dact * act).astype(jnp.bfloat16)
    d_gate = (dact * upper * sig * (1.0 + gate * (1.0 - sig))).astype(jnp.bfloat16)
    inner = (((1,), (1,)), ((), ()))
    d_in = lax.dot_general(d_gate, w_gate, inner, preferred_element_type=jnp.float32)
    d_in = d_in + lax.dot_general(d_up, w_up, inner, preferred_element_type=jnp.float32)
    return d_in.astype(jnp.bfloat16), hidden, d_gate, d_up


def shards(upstream, layer_input, routes, gate_units, gate_weight, up_weight, down_weight):
    received = passed_along(upstream, "section", -1)[0]
    tokens = layer_input[0]
    tok_rows, width = tokens.shape
    count = lax.axis_size("expert")
    experts = count // 2
    expert = lax.axis_index("expert") // 2
    ring = ring_order(count)
    lanes = 128
    units = gate_units[0].astype(jnp.float32) / 256.0
    chosen = routes[0][:, :, None] == jnp.arange(lanes, dtype=jnp.int32)[None, None, :]
    gains = jnp.sum(jnp.where(chosen, units[:, :, None], 0.0), axis=1).astype(jnp.bfloat16)
    packed = jnp.concatenate([tokens, received, gains], axis=1)
    early = jnp.concatenate([tokens, gains], axis=1)
    rows = tok_rows // 2
    w_gate, w_up, w_down = gate_weight[0], up_weight[0], down_weight[0]
    pick = (jnp.arange(lanes, dtype=jnp.int32) == expert).astype(jnp.float32)

    data = packed.shape[1]

    def contribution(block):
        inputs = block[:, :width]
        grads = block[:, width : 2 * width].astype(jnp.float32)
        gain = jnp.sum(block[:, 2 * width : data].astype(jnp.float32) * pick[None, :], axis=1)
        weighted = (gain[:, None] * grads).astype(jnp.bfloat16)
        part, hidden, d_gate, d_up = row_grads(inputs, weighted, w_gate, w_up, w_down)
        kept.append((inputs, weighted, hidden, d_gate, d_up))
        return part[:rows], part[rows:]

    def added(trail, part):
        return (trail.astype(jnp.float32) + part.astype(jnp.float32)).astype(jnp.bfloat16)

    kept = []
    ahead, behind = packed[:rows], packed[rows:]
    early_ahead = along_ring(early[:rows], ring, 1)
    early_behind = along_ring(early[rows:], ring, -1)
    late_ahead = along_ring(received[:rows], ring, 1)
    late_behind = along_ring(received[rows:], ring, -1)
    own = contribution(packed)
    parts = None
    for step in range(1, count):
        if step == 1:
            ahead, behind = (
                jnp.concatenate([e[:, :width], l, e[:, width:]], axis=1)
                for e, l in ((early_ahead, late_ahead), (early_behind, late_behind))
            )
        else:
            ahead, behind = sent_ahead, sent_behind
        if step == 1:
            sums = None
        elif step == 2:
            sums = parts
        else:
            trail = (ahead[:, data:], behind[:, data:])
            sums = (added(trail[0], parts[0]), added(trail[1], parts[1]))
        if sums is None:
            outgoing = (ahead[:, :data], behind[:, :data])
        elif step < count - 1:
            outgoing = (
                jnp.concatenate([ahead[:, :data], sums[0]], axis=1),
                jnp.concatenate([behind[:, :data], sums[1]], axis=1),
            )
        else:
            outgoing = sums
        block = jnp.concatenate([ahead[:, :data], behind[:, :data]], axis=0)
        outgoing, block = lax.optimization_barrier((outgoing, block))
        sent_ahead = along_ring(outgoing[0], ring, 1)
        sent_behind = along_ring(outgoing[1], ring, -1)
        parts = contribution(block)
    trail = (sent_ahead, sent_behind)
    sums = (added(trail[0], parts[0]), added(trail[1], parts[1]))
    total = jnp.concatenate([along_ring(sums[0], ring, 1), along_ring(sums[1], ring, -1)], axis=0)
    total = total.astype(jnp.float32) + jnp.concatenate(own, axis=0).astype(jnp.float32)
    outer = (((0,), (0,)), ((), ()))
    acc = None
    for first, last in ((0, count // 2 + 1), (count // 2 + 1, count - 2), (count - 2, count)):
        inputs, weighted, hidden, d_gate, d_up = (
            jnp.concatenate([k[i] for k in kept[first:last]], axis=0) for i in range(5)
        )
        grads = (
            lax.dot_general(inputs, d_gate, outer, preferred_element_type=jnp.float32),
            lax.dot_general(inputs, d_up, outer, preferred_element_type=jnp.float32),
            lax.dot_general(hidden, weighted, outer, preferred_element_type=jnp.float32),
        )
        acc = grads if acc is None else tuple(a + g for a, g in zip(acc, grads))
    grad_input = (total.astype(jnp.float32) + received.astype(jnp.float32)).astype(jnp.bfloat16)
    g_gate, g_up, g_down = (a.astype(jnp.bfloat16) for a in acc)
    return (grad_input[None], g_gate[None], g_up[None], g_down[None])


def solution(mesh):
    in_specs = (
        P("section", "expert", None),
        P("section", "expert", None),
        P("section", "expert", None),
        P("section", "expert", None),
        P("section", None, "expert"),
        P("section", None, "expert"),
        P("section", "expert", None),
    )
    out_specs = (
        P("section", "expert", None),
        P("section", None, "expert"),
        P("section", None, "expert"),
        P("section", "expert", None),
    )
    return jax.shard_map(shards, mesh=mesh, in_specs=in_specs, out_specs=out_specs, check_vma=False)
```
